32 devices in a mesh: groups: 2 (over y), seq: 4 (over z), head: 4 (over x, core).
Axes of the slice: x: 2, y: 2, z: 4, core: 2. Of those that a mesh axis runs over, the one named last changes fastest.
Arguments:
- inner_acts: bfloat16 [4096, 2560], P(('groups', 'seq'), 'head'), parts along dimension 0, may hold values from -64 to 64
- gate_acts: bfloat16 [4096, 2560], P(('groups', 'seq'), 'head'), parts along dimension 0, may hold values from -6 to 6
- write_map: bfloat16 [2, 4096, 128], P(None, ('groups', 'seq')), parts along dimension 1, may hold values from -6 to 6
- read_map: bfloat16 [2, 4096, 128], P(None, ('groups', 'seq')), parts along dimension 1, may hold values from -0.5 to 0.5
- step_raw: float32 [2, 4096, 40], P(None, ('groups', 'seq'), 'head'), parts along dimension 1, may hold values from -3 to 90.50967
- step_bias: float32 [40], P('head'), may hold values from -7 to -1
- decay_log: float32 [40], P('head'), may hold values from -9 to -1
- skip_gain: float32 [40], P('head'), may hold values from 0.5 to 2
- norm_gain: float32 [2560], P('head'), may hold values from 0.5 to 1.5
- out_weight: bfloat16 [2560, 2560], P('head'), may hold values from -0.125 to 0.125
- residual: bfloat16 [4096, 2560], P(('groups', 'seq'), 'head'), parts along dimension 0, may hold values from -58 to 58
- final_gain: float32 [2560], replicated, may hold values from 0.5 to 1.5
- key_weight: bfloat16 [2560, 2048], P(None, 'head'), may hold values from -0.125 to 0.125
- value_weight: bfloat16 [2560, 2048], P(None, 'head'), may hold values from -0.125 to 0.125
Outputs:
- cross_keys: bfloat16 [4096, 2048], P(('groups', 'seq'), 'head'), parts along dimension 0
- cross_values: bfloat16 [4096, 2048], P(('groups', 'seq'), 'head'), parts along dimension 0
The draws below stay inside these ranges and needn't reach their ends.
There are 2 independent parts, one for each index of `groups`. The reference program is written for one: setup_inputs(seed, part) draws one part's arguments, and reference() takes and returns one part's arrays. A program takes and returns all parts, laid end to end along the dimension named above; an argument that names none is the same for every part. Nothing has to cross between parts.
All inputs are finite; a program needn't handle non-finite values.
Results may differ from the reference program's by a relative error of at most 0.0054.
Values may be sent and summed in bfloat16 or wider, within the bound.
No kernel may reach another device: no remote copies, remote signals or barrier semaphores. Data moves between devices by JAX's collectives and lax.ppermute only.
A program may use at most 128 MiB of HBM per device.

```python
import math
import jax
import jax.numpy as jnp
from jax import lax

D = 2560
HEADS = 40
HEAD_DIM = 64
STATE = 128
STRETCH = 256
NORM_GROUPS = 4
KV_HEADS = 16
KV_DIM = 128
TOK_DEV = 512
SEQ_LEN = 2048


def head_law(key):
    streams = jax.random.split(jax.random.fold_in(key, 71), 4)
    fast_tenths = 4
    fast = jax.random.randint(streams[0], (HEADS,), 0, 10) < fast_tenths
    keeping = jnp.exp(jax.random.uniform(streams[1], (HEADS,), jnp.float32, math.log(0.12), math.log(0.35)))
    memory = jnp.exp(jax.random.uniform(streams[2], (HEADS,), jnp.float32, math.log(25.0), math.log(50.0)))
    slow_log = jnp.log(keeping) - 0.5 * math.log(SEQ_LEN)
    fast_log = -jnp.log(memory * 0.16)
    decays = jnp.where(fast, fast_log, slow_log)
    jitter = jax.random.uniform(streams[3], (HEADS,), jnp.float32, -0.3, 0.3)
    slow_bias = math.log(math.exp(SEQ_LEN ** (-0.5)) - 1.0)
    fast_bias = math.log(math.exp(0.16) - 1.0)
    biases = jnp.where(fast, fast_bias, slow_bias) + jitter
    return (decays, biases)


def token_law(key):
    streams = jax.random.split(jax.random.fold_in(key, 13), 6)
    peak_locations = jax.random.randint(streams[0], (2,), 0, SEQ_LEN)
    permutation_index = jnp.arange(SEQ_LEN)
    spike_amplitude = jnp.any(permutation_index[:, None] == peak_locations[None, :], axis=1)
    spectral_peak = 2.0 * SEQ_LEN ** 0.5
    blocks = SEQ_LEN // TOK_DEV
    position_shifts = jax.random.uniform(streams[1], (2, blocks, HEADS), jnp.float32, -0.7, 0.7)
    position_shifts = jnp.repeat(position_shifts, TOK_DEV, axis=1)
    coarse_estimate = jnp.clip(0.4 * jax.random.normal(streams[2], (2, SEQ_LEN, HEADS), jnp.float32), -1.5, 1.5)
    base = jnp.clip(jax.random.normal(streams[3], (SEQ_LEN, HEADS * HEAD_DIM), jnp.float32), -4.0, 4.0)
    row_low = 0.4
    unprocessed_input = jnp.where(spike_amplitude[None, :, None], spectral_peak, position_shifts + coarse_estimate)
    row_scale = jnp.exp(jax.random.uniform(streams[4], (SEQ_LEN, 1), jnp.float32, math.log(row_low), math.log(4.0)))
    chan_scale = jnp.exp(jax.random.uniform(streams[5], (1, HEADS * HEAD_DIM), jnp.float32, math.log(0.4), math.log(4.0)))
    attenuation_factor = jnp.where(spike_amplitude, spectral_peak, 1.0)[:, None]
    acts = base * row_scale * chan_scale / attenuation_factor
    return (unprocessed_input, acts)


def draw_decay_log(key, part):
    return head_law(key)[0]


def draw_step_bias(key, part):
    return head_law(key)[1]


def draw_step_raw(key, part):
    return token_law(key)[0]


def draw_inner_acts(key, part):
    return token_law(key)[1].astype(jnp.bfloat16)


def draw_residual(key, part):
    streams = jax.random.split(jax.random.fold_in(key, 29), 3)
    base = jnp.clip(jax.random.normal(streams[0], (SEQ_LEN, D), jnp.float32), -4.0, 4.0)
    rows = jnp.exp(jax.random.uniform(streams[1], (SEQ_LEN, 1), jnp.float32, math.log(0.3), math.log(3.0)))
    ramp = jnp.exp(math.log(3.0) * jnp.arange(D, dtype=jnp.float32) / D)[None, :]
    columns = ramp * jnp.exp(jax.random.uniform(streams[2], (1, D), jnp.float32, math.log(0.5), math.log(1.6)))
    return (base * rows * columns).astype(jnp.bfloat16)


def steps_of(stream_key, shape, pieces, smallest, high):
    loudness, own = 1.0, jax.random.fold_in(stream_key, 6)
    for dim, parts in pieces:
        heights = jnp.exp(jax.random.uniform(jax.random.fold_in(own, dim), (parts,), jnp.float32, smallest / len(pieces), high / len(pieces)))
        loudness = loudness * jnp.repeat(heights, shape[dim] // parts).reshape([-1 if axis == dim else 1 for axis in range(len(shape))])
    return loudness


def gaussian(rng, dims, scale, limit, shards=(), held_as=jnp.bfloat16):
    level = steps_of(rng, dims, shards, -0.22, 0.18) if shards else 1.0
    array = jax.random.normal(rng, dims, jnp.float32) * scale * level
    return jnp.minimum(jnp.maximum(array, -limit), limit).astype(held_as)


def setup_inputs(seed: int = 0, part: int = 0) -> dict:
    splits = jax.random.split(jax.random.key(seed), 15)
    part_keys = jax.random.split(jax.random.fold_in(splits[14], part), 15)
    inner_acts = draw_inner_acts(jax.random.fold_in(jax.random.fold_in(splits[14], part), 71), part)
    gate_acts = gaussian(part_keys[1], (SEQ_LEN, HEADS * HEAD_DIM), 1.0, 6.0, ((0, 4), (1, 4)))
    write_map = gaussian(part_keys[2], (2, SEQ_LEN, STATE), 1.0, 6.0, ((1, 4),))
    read_map = gaussian(part_keys[3], (2, SEQ_LEN, STATE), STATE ** -0.5, 0.5, ((1, 4),))
    step_raw = draw_step_raw(jax.random.fold_in(jax.random.fold_in(splits[14], part), 71), part)
    step_bias = draw_step_bias(jax.random.fold_in(splits[14], 71), part)
    decay_log = draw_decay_log(jax.random.fold_in(splits[14], 71), part)
    skip_gain = jnp.clip(jnp.exp(math.log(2.0) - 1.3862944 * jax.random.uniform(splits[7], (HEADS,), jnp.float32) ** steps_of(splits[7], (HEADS,), ((0, 4),), -0.2, 0.2)), 0.5, 2.0)
    norm_gain = jnp.clip(0.5 + 1.0 * jax.random.uniform(splits[8], (HEADS * HEAD_DIM,), jnp.float32) ** steps_of(splits[8], (HEADS * HEAD_DIM,), ((0, 4),), -0.2, 0.2), 0.5, 1.5)
    out_weight = gaussian(splits[9], (HEADS * HEAD_DIM, D), (HEADS * HEAD_DIM) ** -0.5, 0.125, ((0, 4),))
    residual = draw_residual(jax.random.fold_in(jax.random.fold_in(splits[14], part), 71), part)
    final_gain = jnp.clip(jax.random.uniform(splits[11], (D,), jnp.float32, 0.5, 1.5), 0.5, 1.5)
    key_weight = gaussian(splits[12], (D, KV_HEADS * KV_DIM), D ** -0.5, 0.125, ((1, 4),))
    value_weight = gaussian(splits[13], (D, KV_HEADS * KV_DIM), D ** -0.5, 0.125, ((1, 4),))
    return {"inner_acts": inner_acts, "gate_acts": gate_acts, "write_map": write_map, "read_map": read_map, "step_raw": step_raw, "step_bias": step_bias, "decay_log": decay_log, "skip_gain": skip_gain, "norm_gain": norm_gain, "out_weight": out_weight, "residual": residual, "final_gain": final_gain, "key_weight": key_weight, "value_weight": value_weight}


epsilon = 1e-05
highest = lax.Precision.HIGHEST

def block_step(state, acts, writes, reads, steps, rates):
    cum_rate = jnp.cumsum(rates, axis=0)
    along = jnp.transpose(cum_rate)
    permutation_index = jnp.arange(acts.shape[0])
    lower = permutation_index[:, None] >= permutation_index[None, :]
    spans = along[:, :, None] - along[:, None, :]
    decays = jnp.exp(jnp.where(lower[None], spans, -1e+30))
    intersection = jnp.dot(reads, jnp.transpose(writes), preferred_element_type=jnp.float32)
    weights = (intersection[None] * decays * jnp.transpose(steps)[:, None, :]).astype(jnp.bfloat16)
    weights = lax.optimization_barrier(weights)
    within = jnp.einsum('hts,shp->thp', weights.astype(jnp.float32), acts.astype(jnp.float32), precision=highest)
    carried = jnp.einsum('tn,hpn->thp', reads.astype(jnp.float32), state, precision=highest)
    outputs = within + jnp.exp(cum_rate)[:, :, None] * carried
    tail = jnp.exp(cum_rate[-1][None, :] - cum_rate) * steps
    weighted = acts.astype(jnp.float32) * tail[:, :, None]
    new_state = jnp.exp(cum_rate[-1])[:, None, None] * state + jnp.einsum('thp,tn->hpn', weighted, writes.astype(jnp.float32), precision=highest)
    return (outputs, new_state)

def block_scan(acts, writes, reads, steps, rates):
    total = acts.shape[0]
    count = total // STRETCH
    heads = acts.shape[1]
    width = acts.shape[2]
    inputs = (acts.reshape(count, STRETCH, heads, width), writes.reshape(count, STRETCH, -1), reads.reshape(count, STRETCH, -1), steps.reshape(count, STRETCH, heads), rates.reshape(count, STRETCH, heads))
    initial = jnp.zeros((heads, width, writes.shape[1]), jnp.float32)

    def advance(state, block):
        outputs, new_state = block_step(state, *block)
        return (new_state, outputs)
    ending, results = lax.scan(advance, initial, inputs)
    return results.reshape(total, heads, width)

def reference(inner_acts, gate_acts, write_map, read_map, step_raw, step_bias, decay_log, skip_gain, norm_gain, out_weight, residual, final_gain, key_weight, value_weight):
    total = inner_acts.shape[0]
    acts = inner_acts.reshape(total, HEADS, HEAD_DIM)
    decay_rate = -jnp.exp(decay_log)
    steps_fwd = jax.nn.softplus(step_raw[0] + step_bias[None, :])
    steps_bwd = jax.nn.softplus(step_raw[1] + step_bias[None, :])
    forward = block_scan(acts, write_map[0], read_map[0], steps_fwd, steps_fwd * decay_rate[None, :])
    backward = jnp.flip(block_scan(jnp.flip(acts, 0), jnp.flip(write_map[1], 0), jnp.flip(read_map[1], 0), jnp.flip(steps_bwd, 0), jnp.flip(steps_bwd * decay_rate[None, :], 0)), 0)
    summed = forward + backward + skip_gain[None, :, None] * acts.astype(jnp.float32)
    gated = summed.reshape(total, HEADS * HEAD_DIM) * jax.nn.silu(gate_acts.astype(jnp.float32))
    grouped = gated.reshape(total, NORM_GROUPS, -1)
    scaled = grouped * lax.rsqrt(lax.optimization_barrier(jnp.mean(grouped * grouped, axis=2, keepdims=True)) + epsilon)
    mixed = (scaled.reshape(total, -1) * norm_gain[None, :]).astype(jnp.bfloat16)
    encoded = residual.astype(jnp.float32) + jnp.dot(mixed, out_weight, preferred_element_type=jnp.float32)
    normed = (encoded * lax.rsqrt(lax.optimization_barrier(jnp.mean(encoded * encoded, axis=1, keepdims=True)) + epsilon) * final_gain[None, :]).astype(jnp.bfloat16)
    cross_keys = jnp.dot(normed, key_weight, preferred_element_type=jnp.float32).astype(jnp.bfloat16)
    cross_values = jnp.dot(normed, value_weight, preferred_element_type=jnp.float32).astype(jnp.bfloat16)
    return (cross_keys, cross_values)
```

```python
import jax
import jax.numpy as jnp
from jax import lax
from jax.sharding import PartitionSpec as P

STRETCH = 256
NORM_GROUPS = 4


epsilon = 1e-05
highest = lax.Precision.HIGHEST


def passed_along(value, axis, steps):
    count = lax.axis_size(axis)
    first, last = (max(0, -steps), min(count, count - steps))
    if first >= last:
        return jnp.zeros_like(value)
    return lax.ppermute(value, axis, [(source, source + steps) for source in range(first, last)])


def block_parts(acts, writes, reads, steps, rates, reverse):
    tokens, heads, width = acts.shape
    count = tokens // STRETCH
    acts_b = acts.reshape(count, STRETCH, heads, width)
    writes_b = writes.reshape(count, STRETCH, -1)
    reads_b = reads.reshape(count, STRETCH, -1)
    steps_b = steps.reshape(count, STRETCH, heads)
    rates_b = rates.reshape(count, STRETCH, heads)
    cum_rate = lax.cumsum(rates_b, axis=1, reverse=reverse)
    block_total = cum_rate[:, 0] if reverse else cum_rate[:, -1]
    along = jnp.transpose(cum_rate, (0, 2, 1))
    position = jnp.arange(STRETCH)
    if reverse:
        causal = position[:, None] <= position[None, :]
    else:
        causal = position[:, None] >= position[None, :]
    spans = along[:, :, :, None] - along[:, :, None, :]
    decays = jnp.exp(jnp.where(causal[None, None], spans, -1e30))
    intersection = jnp.einsum("btn,bsn->bts", reads_b, writes_b, preferred_element_type=jnp.float32)
    weights = (
        intersection[:, None] * decays * jnp.transpose(steps_b, (0, 2, 1))[:, :, None, :]
    ).astype(jnp.bfloat16)
    within = jnp.einsum("bhts,bshp->bthp", weights, acts_b, preferred_element_type=jnp.float32)
    tail = jnp.exp(block_total[:, None, :] - cum_rate) * steps_b
    weighted = acts_b.astype(jnp.float32) * tail[:, :, :, None]
    ends = jnp.einsum(
        "bshp,bsn->bhpn", weighted, writes_b.astype(jnp.float32), precision=highest
    )
    return within, cum_rate, ends, jnp.exp(block_total)


def chain_blocks(ends, decays, reverse):
    count = ends.shape[0]
    order = range(count - 1, -1, -1) if reverse else range(count)
    state = jnp.zeros_like(ends[0])
    gain = jnp.ones_like(decays[0])
    starts = [None] * count
    gains = [None] * count
    for index in order:
        starts[index] = state
        gains[index] = gain
        state = decays[index][:, None, None] * state + ends[index]
        gain = gain * decays[index]
    return jnp.stack(starts), jnp.stack(gains), state, gain


def relay(state, gain, axis, steps):
    count = lax.axis_size(axis)
    distance = 1
    while distance < count:
        got_state = passed_along(state, axis, distance * steps)
        got_gain = passed_along(gain, axis, distance * steps)
        state = gain[:, None, None] * got_state + state
        gain = gain * got_gain
        distance *= 2
    return passed_along(state, axis, steps)


def direction_out(acts, writes, reads, steps, rates, reverse, axis):
    within, cum_rate, ends, decays = block_parts(acts, writes, reads, steps, rates, reverse)
    starts, gains, own_end, own_gain = chain_blocks(ends, decays, reverse)
    entering = relay(own_end, own_gain, axis, -1 if reverse else 1)
    block_states = starts + gains[:, :, None, None] * entering[None]
    count = within.shape[0]
    reads_b = reads.reshape(count, STRETCH, -1).astype(jnp.float32)
    carried = jnp.einsum("btn,bhpn->bthp", reads_b, block_states, precision=highest)
    outputs = within + jnp.exp(cum_rate)[:, :, :, None] * carried
    return outputs.reshape(acts.shape)


def per_device(
    inner_acts,
    gate_acts,
    write_map,
    read_map,
    step_raw,
    step_bias,
    decay_log,
    skip_gain,
    norm_gain,
    out_weight,
    residual,
    final_gain,
    key_weight,
    value_weight,
):
    tokens = inner_acts.shape[0]
    heads = step_bias.shape[0]
    width = inner_acts.shape[1] // heads
    acts = inner_acts.reshape(tokens, heads, width)
    decay_rate = -jnp.exp(decay_log)
    steps_fwd = jax.nn.softplus(step_raw[0] + step_bias[None, :])
    steps_bwd = jax.nn.softplus(step_raw[1] + step_bias[None, :])
    fwd_all = direction_out(
        acts, write_map[0], read_map[0], steps_fwd, steps_fwd * decay_rate[None, :], False, "seq"
    )
    bwd_all = direction_out(
        acts, write_map[1], read_map[1], steps_bwd, steps_bwd * decay_rate[None, :], True, "seq"
    )
    summed = fwd_all + bwd_all + skip_gain[None, :, None] * acts.astype(jnp.float32)
    gated = summed.reshape(tokens, heads * width) * jax.nn.silu(gate_acts.astype(jnp.float32))
    grouped = gated.reshape(tokens, NORM_GROUPS // lax.axis_size("head"), -1)
    scaled = grouped * lax.rsqrt(jnp.mean(grouped * grouped, axis=2, keepdims=True) + epsilon)
    mixed = (scaled.reshape(tokens, -1) * norm_gain[None, :]).astype(jnp.bfloat16)
    own_width = residual.shape[1]
    offset = lax.axis_index("head") * own_width
    partial_value = jnp.dot(mixed, out_weight, preferred_element_type=jnp.float32)
    own_cols = lax.dynamic_slice_in_dim(partial_value, offset, own_width, 1) + residual.astype(
        jnp.float32
    )
    partial_value = lax.dynamic_update_slice_in_dim(partial_value, own_cols, offset, 1)
    encoded = lax.psum_scatter(partial_value, "head", scatter_dimension=0, tiled=True)
    normed = (
        encoded
        * lax.rsqrt(jnp.mean(encoded * encoded, axis=1, keepdims=True) + epsilon)
        * final_gain[None, :]
    ).astype(jnp.bfloat16)
    normed = lax.all_gather(normed, "head", axis=0, tiled=True)
    key_sum = jnp.dot(normed, key_weight, preferred_element_type=jnp.float32)
    value_sum = jnp.dot(normed, value_weight, preferred_element_type=jnp.float32)
    return (key_sum.astype(jnp.bfloat16), value_sum.astype(jnp.bfloat16))


def solution(mesh):
    placed = (
        P(("groups", "seq"), "head"),
        P(("groups", "seq"), "head"),
        P(None, ("groups", "seq"), None),
        P(None, ("groups", "seq"), None),
        P(None, ("groups", "seq"), "head"),
        P("head"),
        P("head"),
        P("head"),
        P("head"),
        P("head", None),
        P(("groups", "seq"), "head"),
        P(),
        P(None, "head"),
        P(None, "head"),
    )
    return jax.shard_map(
        per_device,
        mesh=mesh,
        in_specs=placed,
        out_specs=(P(("groups", "seq"), "head"), P(("groups", "seq"), "head")),
        check_vma=False,
    )
```

```python
import jax
import jax.numpy as jnp
from jax import lax
from jax.sharding import Mesh, PartitionSpec as P

STRETCH = 256
NORM_GROUPS = 4


epsilon = 1e-05
highest = lax.Precision.HIGHEST


def passed_along(value, axis, steps):
    count = lax.axis_size(axis)
    first, last = (max(0, -steps), min(count, count - steps))
    if first >= last:
        return jnp.zeros_like(value)
    return lax.ppermute(value, axis, [(source, source + steps) for source in range(first, last)])


def block_parts(acts, writes, reads, steps, rates, reverse):
    tokens, heads, width = acts.shape
    count = tokens // STRETCH
    acts_b = acts.reshape(count, STRETCH, heads, width)
    writes_b = writes.reshape(count, STRETCH, -1)
    reads_b = reads.reshape(count, STRETCH, -1)
    steps_b = steps.reshape(count, STRETCH, heads)
    rates_b = rates.reshape(count, STRETCH, heads)
    cum_rate = lax.cumsum(rates_b, axis=1, reverse=reverse)
    block_total = cum_rate[:, 0] if reverse else cum_rate[:, -1]
    along = jnp.transpose(cum_rate, (0, 2, 1))
    position = jnp.arange(STRETCH)
    if reverse:
        causal = position[:, None] <= position[None, :]
    else:
        causal = position[:, None] >= position[None, :]
    spans = along[:, :, :, None] - along[:, :, None, :]
    decays = jnp.exp(jnp.where(causal[None, None], spans, -1e30))
    intersection = jnp.einsum("btn,bsn->bts", reads_b, writes_b, preferred_element_type=jnp.float32)
    weights = (
        intersection[:, None] * decays * jnp.transpose(steps_b, (0, 2, 1))[:, :, None, :]
    ).astype(jnp.bfloat16)
    within = jnp.einsum("bhts,bshp->bthp", weights, acts_b, preferred_element_type=jnp.float32)
    tail = jnp.exp(block_total[:, None, :] - cum_rate) * steps_b
    weighted = acts_b.astype(jnp.float32) * tail[:, :, :, None]
    ends = jnp.einsum(
        "bshp,bsn->bhpn", weighted, writes_b.astype(jnp.float32), precision=highest
    )
    return within, cum_rate, ends, jnp.exp(block_total)


def chain_blocks(ends, decays, reverse):
    count = ends.shape[0]
    order = range(count - 1, -1, -1) if reverse else range(count)
    state = jnp.zeros_like(ends[0])
    gain = jnp.ones_like(decays[0])
    starts = [None] * count
    gains = [None] * count
    for index in order:
        starts[index] = state
        gains[index] = gain
        state = decays[index][:, None, None] * state + ends[index]
        gain = gain * decays[index]
    return jnp.stack(starts), jnp.stack(gains), state, gain


def relay(state, gain, axis, steps):
    count = lax.axis_size(axis)
    distance = 1
    while distance < count:
        got_state = passed_along(state, axis, distance * steps)
        got_gain = passed_along(gain, axis, distance * steps)
        state = gain[:, None, None] * got_state + state
        gain = gain * got_gain
        distance *= 2
    return passed_along(state, axis, steps)


def direction_out(acts, writes, reads, steps, rates, reverse, axis):
    within, cum_rate, ends, decays = block_parts(acts, writes, reads, steps, rates, reverse)
    starts, gains, own_end, own_gain = chain_blocks(ends, decays, reverse)
    entering = relay(own_end, own_gain, axis, -1 if reverse else 1)
    block_states = starts + gains[:, :, None, None] * entering[None]
    count = within.shape[0]
    reads_b = reads.reshape(count, STRETCH, -1).astype(jnp.float32)
    carried = jnp.einsum("btn,bhpn->bthp", reads_b, block_states, precision=highest)
    outputs = within + jnp.exp(cum_rate)[:, :, :, None] * carried
    return outputs.reshape(acts.shape)


def per_device(
    inner_acts,
    gate_acts,
    write_map,
    read_map,
    step_raw,
    step_bias,
    decay_log,
    skip_gain,
    norm_gain,
    out_weight,
    residual,
    final_gain,
    key_weight,
    value_weight,
):
    tokens = inner_acts.shape[0]
    heads = step_bias.shape[0]
    width = inner_acts.shape[1] // heads
    acts = inner_acts.reshape(tokens, heads, width)
    decay_rate = -jnp.exp(decay_log)
    steps_fwd = jax.nn.softplus(step_raw[0] + step_bias[None, :])
    steps_bwd = jax.nn.softplus(step_raw[1] + step_bias[None, :])
    fwd_all = direction_out(
        acts, write_map[0], read_map[0], steps_fwd, steps_fwd * decay_rate[None, :], False, "seq"
    )
    bwd_all = direction_out(
        acts, write_map[1], read_map[1], steps_bwd, steps_bwd * decay_rate[None, :], True, "seq"
    )
    summed = fwd_all + bwd_all + skip_gain[None, :, None] * acts.astype(jnp.float32)
    gated = summed.reshape(tokens, heads * width) * jax.nn.silu(gate_acts.astype(jnp.float32))
    grouped = gated.reshape(tokens, NORM_GROUPS // (lax.axis_size("head_chip") * lax.axis_size("head_core")), -1)
    scaled = grouped * lax.rsqrt(jnp.mean(grouped * grouped, axis=2, keepdims=True) + epsilon)
    mixed = (scaled.reshape(tokens, -1) * norm_gain[None, :]).astype(jnp.bfloat16)
    own_width = residual.shape[1]
    offset = (lax.axis_index("head_chip") * lax.axis_size("head_core") + lax.axis_index("head_core")) * own_width
    partial_value = jnp.dot(mixed, out_weight, preferred_element_type=jnp.float32)
    own_cols = lax.dynamic_slice_in_dim(partial_value, offset, own_width, 1) + residual.astype(
        jnp.float32
    )
    partial_value = lax.dynamic_update_slice_in_dim(partial_value, own_cols, offset, 1)
    encoded = lax.psum_scatter(partial_value, "head_core", scatter_dimension=0, tiled=True)
    encoded = lax.psum_scatter(encoded, "head_chip", scatter_dimension=0, tiled=True)
    normed = (
        encoded
        * lax.rsqrt(jnp.mean(encoded * encoded, axis=1, keepdims=True) + epsilon)
        * final_gain[None, :]
    ).astype(jnp.bfloat16)
    normed = lax.all_gather(normed, "head_chip", axis=0, tiled=True)
    normed = lax.all_gather(normed, "head_core", axis=0, tiled=True)
    key_sum = jnp.dot(normed, key_weight, preferred_element_type=jnp.float32)
    value_sum = jnp.dot(normed, value_weight, preferred_element_type=jnp.float32)
    return (key_sum.astype(jnp.bfloat16), value_sum.astype(jnp.bfloat16))


def split_head(mesh):
    shape = dict(mesh.shape)
    head = shape["head"]
    cores = 2 if head % 2 == 0 else 1
    devices = mesh.devices.reshape(shape["groups"], shape["seq"], head // cores, cores)
    return Mesh(devices, ("groups", "seq", "head_chip", "head_core"))


def solution(mesh):
    mesh = split_head(mesh)
    head = ("head_chip", "head_core")
    placed = (
        P(("groups", "seq"), head),
        P(("groups", "seq"), head),
        P(None, ("groups", "seq"), None),
        P(None, ("groups", "seq"), None),
        P(None, ("groups", "seq"), head),
        P(head),
        P(head),
        P(head),
        P(head),
        P(head, None),
        P(("groups", "seq"), head),
        P(),
        P(None, head),
        P(None, head),
    )
    return jax.shard_map(
        per_device,
        mesh=mesh,
        in_specs=placed,
        out_specs=(P(("groups", "seq"), head), P(("groups", "seq"), head)),
        check_vma=False,
    )
```

```python
import jax
import jax.numpy as jnp
from jax import lax
from jax.sharding import PartitionSpec as P

STRETCH = 256
NORM_GROUPS = 4


epsilon = 1e-05
highest = lax.Precision.HIGHEST


def passed_along(value, axis, steps):
    count = lax.axis_size(axis)
    first, last = (max(0, -steps), min(count, count - steps))
    if first >= last:
        return jnp.zeros_like(value)
    return lax.ppermute(value, axis, [(source, source + steps) for source in range(first, last)])


def block_parts(acts, writes, reads, steps, rates, reverse):
    tokens, heads, width = acts.shape
    count = tokens // STRETCH
    acts_b = acts.reshape(count, STRETCH, heads, width)
    writes_b = writes.reshape(count, STRETCH, -1)
    reads_b = reads.reshape(count, STRETCH, -1)
    steps_b = steps.reshape(count, STRETCH, heads)
    rates_b = rates.reshape(count, STRETCH, heads)
    cum_rate = lax.cumsum(rates_b, axis=1, reverse=reverse)
    block_total = cum_rate[:, 0] if reverse else cum_rate[:, -1]
    along = jnp.transpose(cum_rate, (0, 2, 1))
    position = jnp.arange(STRETCH)
    if reverse:
        causal = position[:, None] <= position[None, :]
    else:
        causal = position[:, None] >= position[None, :]
    spans = along[:, :, :, None] - along[:, :, None, :]
    decays = jnp.exp(jnp.where(causal[None, None], spans, -1e30))
    intersection = jnp.einsum("btn,bsn->bts", reads_b, writes_b, preferred_element_type=jnp.float32)
    weights = (
        intersection[:, None] * decays * jnp.transpose(steps_b, (0, 2, 1))[:, :, None, :]
    ).astype(jnp.bfloat16)
    within = jnp.einsum("bhts,bshp->bthp", weights, acts_b, preferred_element_type=jnp.float32)
    tail = jnp.exp(block_total[:, None, :] - cum_rate) * steps_b
    weighted = acts_b.astype(jnp.float32) * tail[:, :, :, None]
    ends = jnp.einsum(
        "bshp,bsn->bhpn", weighted, writes_b.astype(jnp.float32), precision=highest
    )
    return within, cum_rate, ends, jnp.exp(block_total)


def chain_blocks(ends, decays, reverse):
    count = ends.shape[0]
    order = range(count - 1, -1, -1) if reverse else range(count)
    state = jnp.zeros_like(ends[0])
    gain = jnp.ones_like(decays[0])
    starts = [None] * count
    gains = [None] * count
    for index in order:
        starts[index] = state
        gains[index] = gain
        state = decays[index][:, None, None] * state + ends[index]
        gain = gain * decays[index]
    return jnp.stack(starts), jnp.stack(gains), state, gain


def relay(state, gain, axis, steps):
    count = lax.axis_size(axis)
    if count <= 4:
        entering = jnp.zeros_like(state)
        for _ in range(count - 1):
            entering = passed_along(gain[:, None, None] * entering + state, axis, steps)
        return entering
    distance = 1
    while distance < count:
        got_state = passed_along(state, axis, distance * steps)
        got_gain = passed_along(gain, axis, distance * steps)
        state = gain[:, None, None] * got_state + state
        gain = gain * got_gain
        distance *= 2
    return passed_along(state, axis, steps)


def direction_out(acts, writes, reads, steps, rates, reverse, axis):
    within, cum_rate, ends, decays = block_parts(acts, writes, reads, steps, rates, reverse)
    starts, gains, own_end, own_gain = chain_blocks(ends, decays, reverse)
    entering = relay(own_end, own_gain, axis, -1 if reverse else 1)
    block_states = starts + gains[:, :, None, None] * entering[None]
    count = within.shape[0]
    reads_b = reads.reshape(count, STRETCH, -1).astype(jnp.float32)
    carried = jnp.einsum("btn,bhpn->bthp", reads_b, block_states, precision=highest)
    outputs = within + jnp.exp(cum_rate)[:, :, :, None] * carried
    return outputs.reshape(acts.shape)


def per_device(
    inner_acts,
    gate_acts,
    write_map,
    read_map,
    step_raw,
    step_bias,
    decay_log,
    skip_gain,
    norm_gain,
    out_weight,
    residual,
    final_gain,
    key_weight,
    value_weight,
):
    tokens = inner_acts.shape[0]
    heads = step_bias.shape[0]
    width = inner_acts.shape[1] // heads
    acts = inner_acts.reshape(tokens, heads, width)
    decay_rate = -jnp.exp(decay_log)
    steps_fwd = jax.nn.softplus(step_raw[0] + step_bias[None, :])
    steps_bwd = jax.nn.softplus(step_raw[1] + step_bias[None, :])
    fwd_all = direction_out(
        acts, write_map[0], read_map[0], steps_fwd, steps_fwd * decay_rate[None, :], False, "seq"
    )
    bwd_all = direction_out(
        acts, write_map[1], read_map[1], steps_bwd, steps_bwd * decay_rate[None, :], True, "seq"
    )
    summed = fwd_all + bwd_all + skip_gain[None, :, None] * acts.astype(jnp.float32)
    gated = summed.reshape(tokens, heads * width) * jax.nn.silu(gate_acts.astype(jnp.float32))
    grouped = gated.reshape(tokens, NORM_GROUPS // lax.axis_size("head"), -1)
    scaled = grouped * lax.rsqrt(jnp.mean(grouped * grouped, axis=2, keepdims=True) + epsilon)
    mixed = (scaled.reshape(tokens, -1) * norm_gain[None, :]).astype(jnp.bfloat16)
    own_width = residual.shape[1]
    offset = lax.axis_index("head") * own_width
    partial_value = jnp.dot(mixed, out_weight, preferred_element_type=jnp.float32)
    own_cols = lax.dynamic_slice_in_dim(partial_value, offset, own_width, 1) + residual.astype(
        jnp.float32
    )
    partial_value = lax.dynamic_update_slice_in_dim(partial_value, own_cols, offset, 1)
    encoded = lax.psum_scatter(partial_value, "head", scatter_dimension=0, tiled=True)
    normed = (
        encoded
        * lax.rsqrt(jnp.mean(encoded * encoded, axis=1, keepdims=True) + epsilon)
        * final_gain[None, :]
    ).astype(jnp.bfloat16)
    normed = lax.all_gather(normed, "head", axis=0, tiled=True)
    key_sum = jnp.dot(normed, key_weight, preferred_element_type=jnp.float32)
    value_sum = jnp.dot(normed, value_weight, preferred_element_type=jnp.float32)
    return (key_sum.astype(jnp.bfloat16), value_sum.astype(jnp.bfloat16))


def solution(mesh):
    placed = (
        P(("groups", "seq"), "head"),
        P(("groups", "seq"), "head"),
        P(None, ("groups", "seq"), None),
        P(None, ("groups", "seq"), None),
        P(None, ("groups", "seq"), "head"),
        P("head"),
        P("head"),
        P("head"),
        P("head"),
        P("head", None),
        P(("groups", "seq"), "head"),
        P(),
        P(None, "head"),
        P(None, "head"),
    )
    return jax.shard_map(
        per_device,
        mesh=mesh,
        in_specs=placed,
        out_specs=(P(("groups", "seq"), "head"), P(("groups", "seq"), "head")),
        check_vma=False,
    )
```

```python
import jax
import jax.numpy as jnp
from jax import lax
from jax.sharding import PartitionSpec as P

STRETCH = 256
NORM_GROUPS = 4


epsilon = 1e-05
highest = lax.Precision.HIGHEST


def passed_along(value, axis, steps):
    count = lax.axis_size(axis)
    first, last = (max(0, -steps), min(count, count - steps))
    if first >= last:
        return jnp.zeros_like(value)
    return lax.ppermute(value, axis, [(source, source + steps) for source in range(first, last)])


def block_parts(acts, writes, reads, steps, rates, reverse):
    tokens, heads, width = acts.shape
    count = tokens // STRETCH
    acts_b = acts.reshape(count, STRETCH, heads, width)
    writes_b = writes.reshape(count, STRETCH, -1)
    reads_b = reads.reshape(count, STRETCH, -1)
    steps_b = steps.reshape(count, STRETCH, heads)
    rates_b = rates.reshape(count, STRETCH, heads)
    position = jnp.arange(STRETCH)
    if reverse:
        causal = position[:, None] <= position[None, :]
    else:
        causal = position[:, None] >= position[None, :]
    cum_rate = jnp.einsum(
        "ts,bsh->bth", causal.astype(jnp.float32), rates_b, precision=highest
    )
    block_total = cum_rate[:, 0] if reverse else cum_rate[:, -1]
    along = jnp.transpose(cum_rate, (0, 2, 1))
    spans = along[:, :, :, None] - along[:, :, None, :]
    decays = jnp.exp(jnp.where(causal[None, None], spans, -1e30))
    intersection = jnp.einsum("btn,bsn->bts", reads_b, writes_b, preferred_element_type=jnp.float32)
    weights = (
        intersection[:, None] * decays * jnp.transpose(steps_b, (0, 2, 1))[:, :, None, :]
    ).astype(jnp.bfloat16)
    within = jnp.einsum("bhts,bshp->bthp", weights, acts_b, preferred_element_type=jnp.float32)
    tail = jnp.exp(block_total[:, None, :] - cum_rate) * steps_b
    weighted = acts_b.astype(jnp.float32) * tail[:, :, :, None]
    ends = jnp.einsum(
        "bshp,bsn->bhpn", weighted, writes_b.astype(jnp.float32), precision=highest
    )
    return within, cum_rate, ends, jnp.exp(block_total)


def chain_blocks(ends, decays, reverse):
    count = ends.shape[0]
    order = range(count - 1, -1, -1) if reverse else range(count)
    state = jnp.zeros_like(ends[0])
    gain = jnp.ones_like(decays[0])
    starts = [None] * count
    gains = [None] * count
    for index in order:
        starts[index] = state
        gains[index] = gain
        state = decays[index][:, None, None] * state + ends[index]
        gain = gain * decays[index]
    return jnp.stack(starts), jnp.stack(gains), state, gain


def relay(state, gain, axis, steps):
    count = lax.axis_size(axis)
    if count <= 4:
        entering = jnp.zeros_like(state)
        for _ in range(count - 1):
            entering = passed_along(gain[:, None, None] * entering + state, axis, steps)
        return entering
    distance = 1
    while distance < count:
        got_state = passed_along(state, axis, distance * steps)
        got_gain = passed_along(gain, axis, distance * steps)
        state = gain[:, None, None] * got_state + state
        gain = gain * got_gain
        distance *= 2
    return passed_along(state, axis, steps)


def direction_out(acts, writes, reads, steps, rates, reverse, axis):
    within, cum_rate, ends, decays = block_parts(acts, writes, reads, steps, rates, reverse)
    starts, gains, own_end, own_gain = chain_blocks(ends, decays, reverse)
    entering = relay(own_end, own_gain, axis, -1 if reverse else 1)
    block_states = starts + gains[:, :, None, None] * entering[None]
    count = within.shape[0]
    reads_b = reads.reshape(count, STRETCH, -1).astype(jnp.float32)
    carried = jnp.einsum("btn,bhpn->bthp", reads_b, block_states, precision=highest)
    outputs = within + jnp.exp(cum_rate)[:, :, :, None] * carried
    return outputs.reshape(acts.shape)


def per_device(
    inner_acts,
    gate_acts,
    write_map,
    read_map,
    step_raw,
    step_bias,
    decay_log,
    skip_gain,
    norm_gain,
    out_weight,
    residual,
    final_gain,
    key_weight,
    value_weight,
):
    tokens = inner_acts.shape[0]
    heads = step_bias.shape[0]
    width = inner_acts.shape[1] // heads
    acts = inner_acts.reshape(tokens, heads, width)
    decay_rate = -jnp.exp(decay_log)
    steps_fwd = jax.nn.softplus(step_raw[0] + step_bias[None, :])
    steps_bwd = jax.nn.softplus(step_raw[1] + step_bias[None, :])
    fwd_all = direction_out(
        acts, write_map[0], read_map[0], steps_fwd, steps_fwd * decay_rate[None, :], False, "seq"
    )
    bwd_all = direction_out(
        acts, write_map[1], read_map[1], steps_bwd, steps_bwd * decay_rate[None, :], True, "seq"
    )
    summed = fwd_all + bwd_all + skip_gain[None, :, None] * acts.astype(jnp.float32)
    gated = summed.reshape(tokens, heads * width) * jax.nn.silu(gate_acts.astype(jnp.float32))
    grouped = gated.reshape(tokens, NORM_GROUPS // lax.axis_size("head"), -1)
    scaled = grouped * lax.rsqrt(jnp.mean(grouped * grouped, axis=2, keepdims=True) + epsilon)
    mixed = (scaled.reshape(tokens, -1) * norm_gain[None, :]).astype(jnp.bfloat16)
    own_width = residual.shape[1]
    offset = lax.axis_index("head") * own_width
    chunks = 2 if tokens % (2 * lax.axis_size("head")) == 0 else 1
    rows = tokens // chunks
    keys, values = [], []
    for chunk in range(chunks):
        part = slice(chunk * rows, (chunk + 1) * rows)
        partial_value = jnp.dot(mixed[part], out_weight, preferred_element_type=jnp.float32)
        own_cols = lax.dynamic_slice_in_dim(partial_value, offset, own_width, 1) + residual[
            part
        ].astype(jnp.float32)
        partial_value = lax.dynamic_update_slice_in_dim(partial_value, own_cols, offset, 1)
        encoded = lax.psum_scatter(partial_value, "head", scatter_dimension=0, tiled=True)
        normed = (
            encoded
            * lax.rsqrt(jnp.mean(encoded * encoded, axis=1, keepdims=True) + epsilon)
            * final_gain[None, :]
        ).astype(jnp.bfloat16)
        normed = lax.all_gather(normed, "head", axis=0, tiled=True)
        keys.append(jnp.dot(normed, key_weight, preferred_element_type=jnp.float32).astype(jnp.bfloat16))
        values.append(
            jnp.dot(normed, value_weight, preferred_element_type=jnp.float32).astype(jnp.bfloat16)
        )
    return (jnp.concatenate(keys, axis=0), jnp.concatenate(values, axis=0))


def solution(mesh):
    placed = (
        P(("groups", "seq"), "head"),
        P(("groups", "seq"), "head"),
        P(None, ("groups", "seq"), None),
        P(None, ("groups", "seq"), None),
        P(None, ("groups", "seq"), "head"),
        P("head"),
        P("head"),
        P("head"),
        P("head"),
        P("head", None),
        P(("groups", "seq"), "head"),
        P(),
        P(None, "head"),
        P(None, "head"),
    )
    return jax.shard_map(
        per_device,
        mesh=mesh,
        in_specs=placed,
        out_specs=(P(("groups", "seq"), "head"), P(("groups", "seq"), "head")),
        check_vma=False,
    )
```

```python
import jax
import jax.numpy as jnp
from jax import lax
from jax.sharding import PartitionSpec as P

STRETCH = 256
NORM_GROUPS = 4


epsilon = 1e-05
highest = lax.Precision.HIGHEST


def passed_along(value, axis, steps):
    count = lax.axis_size(axis)
    first, last = (max(0, -steps), min(count, count - steps))
    if first >= last:
        return jnp.zeros_like(value)
    return lax.ppermute(value, axis, [(source, source + steps) for source in range(first, last)])


def block_parts(acts, writes, reads, steps, rates, reverse):
    tokens, heads, width = acts.shape
    count = tokens // STRETCH
    acts_b = acts.reshape(count, STRETCH, heads, width)
    writes_b = writes.reshape(count, STRETCH, -1)
    reads_b = reads.reshape(count, STRETCH, -1)
    steps_b = steps.reshape(count, STRETCH, heads)
    rates_b = rates.reshape(count, STRETCH, heads)
    position = jnp.arange(STRETCH)
    if reverse:
        causal = position[:, None] <= position[None, :]
    else:
        causal = position[:, None] >= position[None, :]
    cum_rate = jnp.einsum(
        "ts,bsh->bth", causal.astype(jnp.float32), rates_b, precision=highest
    )
    block_total = cum_rate[:, 0] if reverse else cum_rate[:, -1]
    along = jnp.transpose(cum_rate, (0, 2, 1))
    spans = along[:, :, :, None] - along[:, :, None, :]
    decays = jnp.exp(jnp.where(causal[None, None], spans, -1e30))
    intersection = jnp.einsum("btn,bsn->bts", reads_b, writes_b, preferred_element_type=jnp.float32)
    weights = (
        intersection[:, None] * decays * jnp.transpose(steps_b, (0, 2, 1))[:, :, None, :]
    ).astype(jnp.bfloat16)
    within = jnp.einsum("bhts,bshp->bthp", weights, acts_b, preferred_element_type=jnp.float32)
    tail = jnp.exp(block_total[:, None, :] - cum_rate) * steps_b
    weighted = acts_b.astype(jnp.float32) * tail[:, :, :, None]
    ends = jnp.einsum(
        "bshp,bsn->bhpn", weighted, writes_b.astype(jnp.float32), precision=highest
    )
    return within, cum_rate, ends, jnp.exp(block_total)


def chain_blocks(ends, decays, reverse):
    count = ends.shape[0]
    order = range(count - 1, -1, -1) if reverse else range(count)
    state = jnp.zeros_like(ends[0])
    gain = jnp.ones_like(decays[0])
    starts = [None] * count
    gains = [None] * count
    for index in order:
        starts[index] = state
        gains[index] = gain
        state = decays[index][:, None, None] * state + ends[index]
        gain = gain * decays[index]
    return jnp.stack(starts), jnp.stack(gains), state, gain


def relay(state, gain, axis, steps):
    count = lax.axis_size(axis)
    if count <= 4:
        entering = jnp.zeros_like(state)
        for _ in range(count - 1):
            entering = passed_along(gain[:, None, None] * entering + state, axis, steps)
        return entering
    distance = 1
    while distance < count:
        got_state = passed_along(state, axis, distance * steps)
        got_gain = passed_along(gain, axis, distance * steps)
        state = gain[:, None, None] * got_state + state
        gain = gain * got_gain
        distance *= 2
    return passed_along(state, axis, steps)


def direction_out(acts, writes, reads, steps, rates, reverse, axis):
    within, cum_rate, ends, decays = block_parts(acts, writes, reads, steps, rates, reverse)
    starts, gains, own_end, own_gain = chain_blocks(ends, decays, reverse)
    entering = relay(own_end, own_gain, axis, -1 if reverse else 1)
    block_states = starts + gains[:, :, None, None] * entering[None]
    count = within.shape[0]
    reads_b = reads.reshape(count, STRETCH, -1).astype(jnp.float32)
    carried = jnp.einsum("btn,bhpn->bthp", reads_b, block_states, precision=highest)
    outputs = within + jnp.exp(cum_rate)[:, :, :, None] * carried
    return outputs.reshape(acts.shape)


def per_device(
    inner_acts,
    gate_acts,
    write_map,
    read_map,
    step_raw,
    step_bias,
    decay_log,
    skip_gain,
    norm_gain,
    out_weight,
    residual,
    final_gain,
    key_weight,
    value_weight,
):
    tokens = inner_acts.shape[0]
    heads = step_bias.shape[0]
    width = inner_acts.shape[1] // heads
    acts = inner_acts.reshape(tokens, heads, width)
    decay_rate = -jnp.exp(decay_log)
    steps_fwd = jax.nn.softplus(step_raw[0] + step_bias[None, :])
    steps_bwd = jax.nn.softplus(step_raw[1] + step_bias[None, :])
    fwd_all = direction_out(
        acts, write_map[0], read_map[0], steps_fwd, steps_fwd * decay_rate[None, :], False, "seq"
    )
    bwd_all = direction_out(
        acts, write_map[1], read_map[1], steps_bwd, steps_bwd * decay_rate[None, :], True, "seq"
    )
    summed = fwd_all + bwd_all + skip_gain[None, :, None] * acts.astype(jnp.float32)
    gated = summed.reshape(tokens, heads * width) * jax.nn.silu(gate_acts.astype(jnp.float32))
    grouped = gated.reshape(tokens, NORM_GROUPS // lax.axis_size("head"), -1)
    scaled = grouped * lax.rsqrt(jnp.mean(grouped * grouped, axis=2, keepdims=True) + epsilon)
    mixed = (scaled.reshape(tokens, -1) * norm_gain[None, :]).astype(jnp.bfloat16)
    own_width = residual.shape[1]
    own_block = jnp.arange(out_weight.shape[1]) // own_width == lax.axis_index("head")
    spread = jnp.tile(residual.astype(jnp.float32), (1, out_weight.shape[1] // own_width))
    partial_value = jnp.dot(mixed, out_weight, preferred_element_type=jnp.float32)
    partial_value = partial_value + jnp.where(own_block[None, :], spread, 0.0)
    encoded = lax.psum_scatter(partial_value, "head", scatter_dimension=0, tiled=True)
    normed = (
        encoded
        * lax.rsqrt(jnp.mean(encoded * encoded, axis=1, keepdims=True) + epsilon)
        * final_gain[None, :]
    ).astype(jnp.bfloat16)
    normed = lax.all_gather(normed, "head", axis=0, tiled=True)
    key_sum = jnp.dot(normed, key_weight, preferred_element_type=jnp.float32)
    value_sum = jnp.dot(normed, value_weight, preferred_element_type=jnp.float32)
    return (key_sum.astype(jnp.bfloat16), value_sum.astype(jnp.bfloat16))


def solution(mesh):
    placed = (
        P(("groups", "seq"), "head"),
        P(("groups", "seq"), "head"),
        P(None, ("groups", "seq"), None),
        P(None, ("groups", "seq"), None),
        P(None, ("groups", "seq"), "head"),
        P("head"),
        P("head"),
        P("head"),
        P("head"),
        P("head", None),
        P(("groups", "seq"), "head"),
        P(),
        P(None, "head"),
        P(None, "head"),
    )
    return jax.shard_map(
        per_device,
        mesh=mesh,
        in_specs=placed,
        out_specs=(P(("groups", "seq"), "head"), P(("groups", "seq"), "head")),
        check_vma=False,
    )
```

```python
import jax
import jax.numpy as jnp
from jax import lax
from jax.sharding import PartitionSpec as P

STRETCH = 256
NORM_GROUPS = 4


epsilon = 1e-05
highest = lax.Precision.HIGHEST


def passed_along(value, axis, steps):
    count = lax.axis_size(axis)
    first, last = (max(0, -steps), min(count, count - steps))
    if first >= last:
        return jnp.zeros_like(value)
    return lax.ppermute(value, axis, [(source, source + steps) for source in range(first, last)])


def block_parts(acts, writes, reads, steps, rates, reverse):
    tokens, heads, width = acts.shape
    count = tokens // STRETCH
    acts_b = acts.reshape(count, STRETCH, heads, width)
    writes_b = writes.reshape(count, STRETCH, -1)
    reads_b = reads.reshape(count, STRETCH, -1)
    steps_b = steps.reshape(count, STRETCH, heads)
    rates_b = rates.reshape(count, STRETCH, heads)
    position = jnp.arange(STRETCH)
    if reverse:
        causal = position[:, None] <= position[None, :]
    else:
        causal = position[:, None] >= position[None, :]
    cum_rate = jnp.einsum(
        "ts,bsh->bth", causal.astype(jnp.float32), rates_b, precision=highest
    )
    block_total = cum_rate[:, 0] if reverse else cum_rate[:, -1]
    along = jnp.transpose(cum_rate, (0, 2, 1))
    spans = along[:, :, :, None] - along[:, :, None, :]
    decays = jnp.exp(jnp.where(causal[None, None], spans, -1e30))
    intersection = jnp.einsum("btn,bsn->bts", reads_b, writes_b, preferred_element_type=jnp.float32)
    weights = (
        intersection[:, None] * decays * jnp.transpose(steps_b, (0, 2, 1))[:, :, None, :]
    ).astype(jnp.bfloat16)
    within = jnp.einsum("bhts,bshp->bthp", weights, acts_b, preferred_element_type=jnp.float32)
    tail = jnp.exp(block_total[:, None, :] - cum_rate) * steps_b
    weighted = (acts_b.astype(jnp.float32) * tail[:, :, :, None]).reshape(count, STRETCH, -1)
    ends = jnp.einsum(
        "bsn,bsc->bnc", writes_b.astype(jnp.float32), weighted, precision=highest
    )
    spread = jnp.repeat(jnp.exp(block_total), width, axis=1)
    return within, cum_rate, ends, spread


def chain_blocks(ends, decays, reverse):
    count = ends.shape[0]
    order = range(count - 1, -1, -1) if reverse else range(count)
    state = jnp.zeros_like(ends[0])
    gain = jnp.ones_like(decays[0])
    starts = [None] * count
    gains = [None] * count
    for index in order:
        starts[index] = state
        gains[index] = gain
        state = decays[index][None, :] * state + ends[index]
        gain = gain * decays[index]
    return jnp.stack(starts), jnp.stack(gains), state, gain


def relay(state, gain, axis, steps):
    count = lax.axis_size(axis)
    if count <= 4:
        entering = jnp.zeros_like(state)
        for _ in range(count - 1):
            entering = passed_along(gain[None, :] * entering + state, axis, steps)
        return entering
    distance = 1
    while distance < count:
        got_state = passed_along(state, axis, distance * steps)
        got_gain = passed_along(gain, axis, distance * steps)
        state = gain[None, :] * got_state + state
        gain = gain * got_gain
        distance *= 2
    return passed_along(state, axis, steps)


def direction_out(acts, writes, reads, steps, rates, reverse, axis):
    within, cum_rate, ends, decays = block_parts(acts, writes, reads, steps, rates, reverse)
    starts, gains, own_end, own_gain = chain_blocks(ends, decays, reverse)
    entering = relay(own_end, own_gain, axis, -1 if reverse else 1)
    block_states = starts + gains[:, None, :] * entering[None]
    count, _, heads, width = within.shape
    reads_b = reads.reshape(count, STRETCH, -1).astype(jnp.float32)
    carried = jnp.einsum("btn,bnc->btc", reads_b, block_states, precision=highest)
    carried = carried.reshape(count, STRETCH, heads, width)
    outputs = within + jnp.exp(cum_rate)[:, :, :, None] * carried
    return outputs.reshape(acts.shape)


def per_device(
    inner_acts,
    gate_acts,
    write_map,
    read_map,
    step_raw,
    step_bias,
    decay_log,
    skip_gain,
    norm_gain,
    out_weight,
    residual,
    final_gain,
    key_weight,
    value_weight,
):
    tokens = inner_acts.shape[0]
    heads = step_bias.shape[0]
    width = inner_acts.shape[1] // heads
    acts = inner_acts.reshape(tokens, heads, width)
    decay_rate = -jnp.exp(decay_log)
    steps_fwd = jax.nn.softplus(step_raw[0] + step_bias[None, :])
    steps_bwd = jax.nn.softplus(step_raw[1] + step_bias[None, :])
    fwd_all = direction_out(
        acts, write_map[0], read_map[0], steps_fwd, steps_fwd * decay_rate[None, :], False, "seq"
    )
    bwd_all = direction_out(
        acts, write_map[1], read_map[1], steps_bwd, steps_bwd * decay_rate[None, :], True, "seq"
    )
    summed = fwd_all + bwd_all + skip_gain[None, :, None] * acts.astype(jnp.float32)
    gated = summed.reshape(tokens, heads * width) * jax.nn.silu(gate_acts.astype(jnp.float32))
    grouped = gated.reshape(tokens, NORM_GROUPS // lax.axis_size("head"), -1)
    scaled = grouped * lax.rsqrt(jnp.mean(grouped * grouped, axis=2, keepdims=True) + epsilon)
    mixed = (scaled.reshape(tokens, -1) * norm_gain[None, :]).astype(jnp.bfloat16)
    own_width = residual.shape[1]
    own_block = jnp.arange(out_weight.shape[1]) // own_width == lax.axis_index("head")
    spread = jnp.tile(residual.astype(jnp.float32), (1, out_weight.shape[1] // own_width))
    partial_value = jnp.dot(mixed, out_weight, preferred_element_type=jnp.float32)
    partial_value = partial_value + jnp.where(own_block[None, :], spread, 0.0)
    encoded = lax.psum_scatter(partial_value, "head", scatter_dimension=0, tiled=True)
    normed = (
        encoded
        * lax.rsqrt(jnp.mean(encoded * encoded, axis=1, keepdims=True) + epsilon)
        * final_gain[None, :]
    ).astype(jnp.bfloat16)
    normed = lax.all_gather(normed, "head", axis=0, tiled=True)
    key_sum = jnp.dot(normed, key_weight, preferred_element_type=jnp.float32)
    value_sum = jnp.dot(normed, value_weight, preferred_element_type=jnp.float32)
    return (key_sum.astype(jnp.bfloat16), value_sum.astype(jnp.bfloat16))


def solution(mesh):
    placed = (
        P(("groups", "seq"), "head"),
        P(("groups", "seq"), "head"),
        P(None, ("groups", "seq"), None),
        P(None, ("groups", "seq"), None),
        P(None, ("groups", "seq"), "head"),
        P("head"),
        P("head"),
        P("head"),
        P("head"),
        P("head", None),
        P(("groups", "seq"), "head"),
        P(),
        P(None, "head"),
        P(None, "head"),
    )
    return jax.shard_map(
        per_device,
        mesh=mesh,
        in_specs=placed,
        out_specs=(P(("groups", "seq"), "head"), P(("groups", "seq"), "head")),
        check_vma=False,
    )
```

```python
import jax
import jax.numpy as jnp
from jax import lax
from jax.sharding import PartitionSpec as P

STRETCH = 256
NORM_GROUPS = 4


epsilon = 1e-05
highest = lax.Precision.HIGHEST


def passed_along(value, axis, steps):
    count = lax.axis_size(axis)
    first, last = (max(0, -steps), min(count, count - steps))
    if first >= last:
        return jnp.zeros_like(value)
    return lax.ppermute(value, axis, [(source, source + steps) for source in range(first, last)])


def block_parts(acts, writes, reads, steps, rates, reverse):
    tokens, heads, width = acts.shape
    count = tokens // STRETCH
    acts_b = acts.reshape(count, STRETCH, heads, width)
    writes_b = writes.reshape(count, STRETCH, -1)
    reads_b = reads.reshape(count, STRETCH, -1)
    steps_b = steps.reshape(count, STRETCH, heads)
    rates_b = rates.reshape(count, STRETCH, heads)
    position = jnp.arange(STRETCH)
    if reverse:
        causal = position[:, None] <= position[None, :]
    else:
        causal = position[:, None] >= position[None, :]
    cum_rate = jnp.einsum(
        "ts,bsh->bth", causal.astype(jnp.float32), rates_b, precision=highest
    )
    block_total = cum_rate[:, 0] if reverse else cum_rate[:, -1]
    along = jnp.transpose(cum_rate, (0, 2, 1))
    spans = along[:, :, :, None] - along[:, :, None, :]
    decays = jnp.exp(jnp.where(causal[None, None], spans, -1e30))
    intersection = jnp.einsum("btn,bsn->bts", reads_b, writes_b, preferred_element_type=jnp.float32)
    weights = (
        intersection[:, None] * decays * jnp.transpose(steps_b, (0, 2, 1))[:, :, None, :]
    ).astype(jnp.bfloat16)
    within = jnp.einsum("bhts,bshp->bthp", weights, acts_b, preferred_element_type=jnp.float32)
    tail = jnp.exp(block_total[:, None, :] - cum_rate) * steps_b
    weighted = acts_b.astype(jnp.float32) * tail[:, :, :, None]
    ends = jnp.einsum(
        "bshp,bsn->bhpn", weighted, writes_b.astype(jnp.float32), precision=highest
    )
    return within, cum_rate, ends, jnp.exp(block_total)


def chain_blocks(ends, decays, reverse):
    count = ends.shape[0]
    order = range(count - 1, -1, -1) if reverse else range(count)
    state = jnp.zeros_like(ends[0])
    gain = jnp.ones_like(decays[0])
    starts = [None] * count
    gains = [None] * count
    for index in order:
        starts[index] = state
        gains[index] = gain
        state = decays[index][:, None, None] * state + ends[index]
        gain = gain * decays[index]
    return jnp.stack(starts), jnp.stack(gains), state, gain


def relay(state, gain, axis, steps):
    count = lax.axis_size(axis)
    if count <= 4:
        entering = jnp.zeros_like(state)
        for _ in range(count - 1):
            entering = passed_along(gain[:, None, None] * entering + state, axis, steps)
        return entering
    distance = 1
    while distance < count:
        got_state = passed_along(state, axis, distance * steps)
        got_gain = passed_along(gain, axis, distance * steps)
        state = gain[:, None, None] * got_state + state
        gain = gain * got_gain
        distance *= 2
    return passed_along(state, axis, steps)


def gathered_entry(state, gain, axis):
    count = lax.axis_size(axis)
    me = lax.axis_index(axis)
    heads = state.shape[0]
    flat = state.reshape(heads, -1)
    packed = jnp.concatenate([flat, jnp.broadcast_to(gain[:, None], (heads, 128))], axis=1)
    every = lax.all_gather(packed, axis)
    total = jnp.zeros_like(flat)
    carry = jnp.ones_like(gain)
    for source in range(count - 1, -1, -1):
        take = source < me
        total = total + jnp.where(take, carry, 0.0)[:, None] * every[source, :, : flat.shape[1]]
        carry = jnp.where(take, carry * every[source, :, flat.shape[1]], carry)
    return total.reshape(state.shape)


def direction_out(acts, writes, reads, steps, rates, reverse, axis):
    within, cum_rate, ends, decays = block_parts(acts, writes, reads, steps, rates, reverse)
    starts, gains, own_end, own_gain = chain_blocks(ends, decays, reverse)
    if reverse:
        entering = relay(own_end, own_gain, axis, -1)
    else:
        entering = gathered_entry(own_end, own_gain, axis)
    block_states = starts + gains[:, :, None, None] * entering[None]
    count = within.shape[0]
    reads_b = reads.reshape(count, STRETCH, -1).astype(jnp.float32)
    carried = jnp.einsum("btn,bhpn->bthp", reads_b, block_states, precision=highest)
    outputs = within + jnp.exp(cum_rate)[:, :, :, None] * carried
    return outputs.reshape(acts.shape)


def per_device(
    inner_acts,
    gate_acts,
    write_map,
    read_map,
    step_raw,
    step_bias,
    decay_log,
    skip_gain,
    norm_gain,
    out_weight,
    residual,
    final_gain,
    key_weight,
    value_weight,
):
    tokens = inner_acts.shape[0]
    heads = step_bias.shape[0]
    width = inner_acts.shape[1] // heads
    acts = inner_acts.reshape(tokens, heads, width)
    decay_rate = -jnp.exp(decay_log)
    steps_fwd = jax.nn.softplus(step_raw[0] + step_bias[None, :])
    steps_bwd = jax.nn.softplus(step_raw[1] + step_bias[None, :])
    fwd_all = direction_out(
        acts, write_map[0], read_map[0], steps_fwd, steps_fwd * decay_rate[None, :], False, "seq"
    )
    bwd_all = direction_out(
        acts, write_map[1], read_map[1], steps_bwd, steps_bwd * decay_rate[None, :], True, "seq"
    )
    summed = fwd_all + bwd_all + skip_gain[None, :, None] * acts.astype(jnp.float32)
    gated = summed.reshape(tokens, heads * width) * jax.nn.silu(gate_acts.astype(jnp.float32))
    grouped = gated.reshape(tokens, NORM_GROUPS // lax.axis_size("head"), -1)
    scaled = grouped * lax.rsqrt(jnp.mean(grouped * grouped, axis=2, keepdims=True) + epsilon)
    mixed = (scaled.reshape(tokens, -1) * norm_gain[None, :]).astype(jnp.bfloat16)
    own_width = residual.shape[1]
    own_block = jnp.arange(out_weight.shape[1]) // own_width == lax.axis_index("head")
    spread = jnp.tile(residual.astype(jnp.float32), (1, out_weight.shape[1] // own_width))
    partial_value = jnp.dot(mixed, out_weight, preferred_element_type=jnp.float32)
    partial_value = partial_value + jnp.where(own_block[None, :], spread, 0.0)
    encoded = lax.psum_scatter(partial_value, "head", scatter_dimension=0, tiled=True)
    normed = (
        encoded
        * lax.rsqrt(jnp.mean(encoded * encoded, axis=1, keepdims=True) + epsilon)
        * final_gain[None, :]
    ).astype(jnp.bfloat16)
    normed = lax.all_gather(normed, "head", axis=0, tiled=True)
    key_sum = jnp.dot(normed, key_weight, preferred_element_type=jnp.float32)
    value_sum = jnp.dot(normed, value_weight, preferred_element_type=jnp.float32)
    return (key_sum.astype(jnp.bfloat16), value_sum.astype(jnp.bfloat16))


def solution(mesh):
    placed = (
        P(("groups", "seq"), "head"),
        P(("groups", "seq"), "head"),
        P(None, ("groups", "seq"), None),
        P(None, ("groups", "seq"), None),
        P(None, ("groups", "seq"), "head"),
        P("head"),
        P("head"),
        P("head"),
        P("head"),
        P("head", None),
        P(("groups", "seq"), "head"),
        P(),
        P(None, "head"),
        P(None, "head"),
    )
    return jax.shard_map(
        per_device,
        mesh=mesh,
        in_specs=placed,
        out_specs=(P(("groups", "seq"), "head"), P(("groups", "seq"), "head")),
        check_vma=False,
    )
```

```python
import jax
import jax.numpy as jnp
from jax import lax
from jax.sharding import PartitionSpec as P

STRETCH = 256
NORM_GROUPS = 4


epsilon = 1e-05
highest = lax.Precision.HIGHEST


def passed_along(value, axis, steps):
    count = lax.axis_size(axis)
    first, last = (max(0, -steps), min(count, count - steps))
    if first >= last:
        return jnp.zeros_like(value)
    return lax.ppermute(value, axis, [(source, source + steps) for source in range(first, last)])


def block_parts(acts, writes, reads, steps, rates, reverse):
    tokens, heads, width = acts.shape
    count = tokens // STRETCH
    acts_b = acts.reshape(count, STRETCH, heads, width)
    writes_b = writes.reshape(count, STRETCH, -1)
    reads_b = reads.reshape(count, STRETCH, -1)
    steps_b = steps.reshape(count, STRETCH, heads)
    rates_b = rates.reshape(count, STRETCH, heads)
    position = jnp.arange(STRETCH)
    if reverse:
        causal = position[:, None] <= position[None, :]
    else:
        causal = position[:, None] >= position[None, :]
    cum_rate = jnp.einsum(
        "ts,bsh->bth", causal.astype(jnp.float32), rates_b, precision=highest
    )
    block_total = cum_rate[:, 0] if reverse else cum_rate[:, -1]
    along = jnp.transpose(cum_rate, (0, 2, 1))
    spans = along[:, :, :, None] - along[:, :, None, :]
    decays = jnp.exp(jnp.where(causal[None, None], spans, -1e30))
    intersection = jnp.einsum("btn,bsn->bts", reads_b, writes_b, preferred_element_type=jnp.float32)
    weights = (
        intersection[:, None] * decays * jnp.transpose(steps_b, (0, 2, 1))[:, :, None, :]
    ).astype(jnp.bfloat16)
    weights = jnp.transpose(weights, (0, 2, 1, 3)).reshape(count, STRETCH, heads * STRETCH)
    same_head = jnp.arange(heads)[:, None, None, None] == jnp.arange(heads)[None, None, :, None]
    diagonal = jnp.where(same_head[None], acts_b[:, None], jnp.zeros((), acts_b.dtype))
    diagonal = diagonal.reshape(count, heads * STRETCH, heads * width)
    within = jnp.einsum("btk,bkc->btc", weights, diagonal, preferred_element_type=jnp.float32)
    within = within.reshape(count, STRETCH, heads, width)
    tail = jnp.exp(block_total[:, None, :] - cum_rate) * steps_b
    weighted = acts_b.astype(jnp.float32) * tail[:, :, :, None]
    ends = jnp.einsum(
        "bshp,bsn->bhpn", weighted, writes_b.astype(jnp.float32), precision=highest
    )
    return within, cum_rate, ends, jnp.exp(block_total)


def chain_blocks(ends, decays, reverse):
    count = ends.shape[0]
    order = range(count - 1, -1, -1) if reverse else range(count)
    state = jnp.zeros_like(ends[0])
    gain = jnp.ones_like(decays[0])
    starts = [None] * count
    gains = [None] * count
    for index in order:
        starts[index] = state
        gains[index] = gain
        state = decays[index][:, None, None] * state + ends[index]
        gain = gain * decays[index]
    return jnp.stack(starts), jnp.stack(gains), state, gain


def relay(state, gain, axis, steps):
    count = lax.axis_size(axis)
    if count <= 4:
        entering = jnp.zeros_like(state)
        for _ in range(count - 1):
            entering = passed_along(gain[:, None, None] * entering + state, axis, steps)
        return entering
    distance = 1
    while distance < count:
        got_state = passed_along(state, axis, distance * steps)
        got_gain = passed_along(gain, axis, distance * steps)
        state = gain[:, None, None] * got_state + state
        gain = gain * got_gain
        distance *= 2
    return passed_along(state, axis, steps)


def direction_out(acts, writes, reads, steps, rates, reverse, axis):
    within, cum_rate, ends, decays = block_parts(acts, writes, reads, steps, rates, reverse)
    starts, gains, own_end, own_gain = chain_blocks(ends, decays, reverse)
    entering = relay(own_end, own_gain, axis, -1 if reverse else 1)
    block_states = starts + gains[:, :, None, None] * entering[None]
    count = within.shape[0]
    reads_b = reads.reshape(count, STRETCH, -1).astype(jnp.float32)
    carried = jnp.einsum("btn,bhpn->bthp", reads_b, block_states, precision=highest)
    outputs = within + jnp.exp(cum_rate)[:, :, :, None] * carried
    return outputs.reshape(acts.shape)


def per_device(
    inner_acts,
    gate_acts,
    write_map,
    read_map,
    step_raw,
    step_bias,
    decay_log,
    skip_gain,
    norm_gain,
    out_weight,
    residual,
    final_gain,
    key_weight,
    value_weight,
):
    tokens = inner_acts.shape[0]
    heads = step_bias.shape[0]
    width = inner_acts.shape[1] // heads
    acts = inner_acts.reshape(tokens, heads, width)
    decay_rate = -jnp.exp(decay_log)
    steps_fwd = jax.nn.softplus(step_raw[0] + step_bias[None, :])
    steps_bwd = jax.nn.softplus(step_raw[1] + step_bias[None, :])
    fwd_all = direction_out(
        acts, write_map[0], read_map[0], steps_fwd, steps_fwd * decay_rate[None, :], False, "seq"
    )
    bwd_all = direction_out(
        acts, write_map[1], read_map[1], steps_bwd, steps_bwd * decay_rate[None, :], True, "seq"
    )
    summed = fwd_all + bwd_all + skip_gain[None, :, None] * acts.astype(jnp.float32)
    gated = summed.reshape(tokens, heads * width) * jax.nn.silu(gate_acts.astype(jnp.float32))
    grouped = gated.reshape(tokens, NORM_GROUPS // lax.axis_size("head"), -1)
    scaled = grouped * lax.rsqrt(jnp.mean(grouped * grouped, axis=2, keepdims=True) + epsilon)
    mixed = (scaled.reshape(tokens, -1) * norm_gain[None, :]).astype(jnp.bfloat16)
    own_width = residual.shape[1]
    own_block = jnp.arange(out_weight.shape[1]) // own_width == lax.axis_index("head")
    spread = jnp.tile(residual.astype(jnp.float32), (1, out_weight.shape[1] // own_width))
    partial_value = jnp.dot(mixed, out_weight, preferred_element_type=jnp.float32)
    partial_value = partial_value + jnp.where(own_block[None, :], spread, 0.0)
    encoded = lax.psum_scatter(partial_value, "head", scatter_dimension=0, tiled=True)
    normed = (
        encoded
        * lax.rsqrt(jnp.mean(encoded * encoded, axis=1, keepdims=True) + epsilon)
        * final_gain[None, :]
    ).astype(jnp.bfloat16)
    normed = lax.all_gather(normed, "head", axis=0, tiled=True)
    key_sum = jnp.dot(normed, key_weight, preferred_element_type=jnp.float32)
    value_sum = jnp.dot(normed, value_weight, preferred_element_type=jnp.float32)
    return (key_sum.astype(jnp.bfloat16), value_sum.astype(jnp.bfloat16))


def solution(mesh):
    placed = (
        P(("groups", "seq"), "head"),
        P(("groups", "seq"), "head"),
        P(None, ("groups", "seq"), None),
        P(None, ("groups", "seq"), None),
        P(None, ("groups", "seq"), "head"),
        P("head"),
        P("head"),
        P("head"),
        P("head"),
        P("head", None),
        P(("groups", "seq"), "head"),
        P(),
        P(None, "head"),
        P(None, "head"),
    )
    return jax.shard_map(
        per_device,
        mesh=mesh,
        in_specs=placed,
        out_specs=(P(("groups", "seq"), "head"), P(("groups", "seq"), "head")),
        check_vma=False,
    )
```

```python
import jax
import jax.numpy as jnp
from jax import lax
from jax.sharding import PartitionSpec as P

STRETCH = 256
NORM_GROUPS = 4


epsilon = 1e-05
highest = lax.Precision.HIGHEST


def passed_along(value, axis, steps):
    count = lax.axis_size(axis)
    first, last = (max(0, -steps), min(count, count - steps))
    if first >= last:
        return jnp.zeros_like(value)
    return lax.ppermute(value, axis, [(source, source + steps) for source in range(first, last)])


def block_parts(acts, writes, reads, steps, rates):
    tokens, heads, width = acts.shape
    count = tokens // STRETCH
    acts_b = acts.reshape(count, STRETCH, heads, width)
    writes_b = writes.reshape(2, count, STRETCH, -1)
    reads_b = reads.reshape(2, count, STRETCH, -1)
    steps_b = steps.reshape(2, count, STRETCH, heads)
    rates_b = rates.reshape(2, count, STRETCH, heads)
    position = jnp.arange(STRETCH)
    causal = jnp.stack(
        [position[:, None] >= position[None, :], position[:, None] <= position[None, :]]
    )
    cum_rate = jnp.einsum(
        "dts,dbsh->dbth", causal.astype(jnp.float32), rates_b, precision=highest
    )
    block_total = jnp.stack([cum_rate[0, :, -1], cum_rate[1, :, 0]])
    along = jnp.transpose(cum_rate, (0, 1, 3, 2))
    spans = along[..., :, None] - along[..., None, :]
    decays = jnp.exp(jnp.where(causal[:, None, None], spans, -1e30))
    intersection = jnp.einsum(
        "dbtn,dbsn->dbts", reads_b, writes_b, preferred_element_type=jnp.float32
    )
    weights = (
        intersection[:, :, None]
        * decays
        * jnp.transpose(steps_b, (0, 1, 3, 2))[:, :, :, None, :]
    ).astype(jnp.bfloat16)
    within = jnp.einsum(
        "dbhts,bshp->dbthp", weights, acts_b, preferred_element_type=jnp.float32
    )
    tail = jnp.exp(block_total[:, :, None, :] - cum_rate) * steps_b
    weighted = acts_b.astype(jnp.float32)[None] * tail[..., None]
    ends = jnp.einsum(
        "dbshp,dbsn->dbhpn", weighted, writes_b.astype(jnp.float32), precision=highest
    )
    return within, cum_rate, ends, jnp.exp(block_total)


def chain_blocks(ends, decays, reverse):
    count = ends.shape[0]
    order = range(count - 1, -1, -1) if reverse else range(count)
    state = jnp.zeros_like(ends[0])
    gain = jnp.ones_like(decays[0])
    starts = [None] * count
    gains = [None] * count
    for index in order:
        starts[index] = state
        gains[index] = gain
        state = decays[index][:, None, None] * state + ends[index]
        gain = gain * decays[index]
    return jnp.stack(starts), jnp.stack(gains), state, gain


def relay(state, gain, axis, steps):
    count = lax.axis_size(axis)
    if count <= 4:
        entering = jnp.zeros_like(state)
        for _ in range(count - 1):
            entering = passed_along(gain[:, None, None] * entering + state, axis, steps)
        return entering
    distance = 1
    while distance < count:
        got_state = passed_along(state, axis, distance * steps)
        got_gain = passed_along(gain, axis, distance * steps)
        state = gain[:, None, None] * got_state + state
        gain = gain * got_gain
        distance *= 2
    return passed_along(state, axis, steps)


def both_directions(acts, writes, reads, steps, rates, axis):
    within, cum_rate, ends, decays = block_parts(acts, writes, reads, steps, rates)
    block_states = []
    for direction, reverse in ((0, False), (1, True)):
        starts, gains, own_end, own_gain = chain_blocks(ends[direction], decays[direction], reverse)
        entering = relay(own_end, own_gain, axis, -1 if reverse else 1)
        block_states.append(starts + gains[:, :, None, None] * entering[None])
    block_states = jnp.stack(block_states)
    count = within.shape[1]
    reads_b = reads.reshape(2, count, STRETCH, -1).astype(jnp.float32)
    carried = jnp.einsum("dbtn,dbhpn->dbthp", reads_b, block_states, precision=highest)
    outputs = within + jnp.exp(cum_rate)[..., None] * carried
    return outputs.reshape((2,) + acts.shape)


def per_device(
    inner_acts,
    gate_acts,
    write_map,
    read_map,
    step_raw,
    step_bias,
    decay_log,
    skip_gain,
    norm_gain,
    out_weight,
    residual,
    final_gain,
    key_weight,
    value_weight,
):
    tokens = inner_acts.shape[0]
    heads = step_bias.shape[0]
    width = inner_acts.shape[1] // heads
    acts = inner_acts.reshape(tokens, heads, width)
    decay_rate = -jnp.exp(decay_log)
    steps_both = jax.nn.softplus(step_raw + step_bias[None, None, :])
    outputs = both_directions(
        acts, write_map, read_map, steps_both, steps_both * decay_rate[None, None, :], "seq"
    )
    summed = outputs[0] + outputs[1] + skip_gain[None, :, None] * acts.astype(jnp.float32)
    gated = summed.reshape(tokens, heads * width) * jax.nn.silu(gate_acts.astype(jnp.float32))
    grouped = gated.reshape(tokens, NORM_GROUPS // lax.axis_size("head"), -1)
    scaled = grouped * lax.rsqrt(jnp.mean(grouped * grouped, axis=2, keepdims=True) + epsilon)
    mixed = (scaled.reshape(tokens, -1) * norm_gain[None, :]).astype(jnp.bfloat16)
    own_width = residual.shape[1]
    own_block = jnp.arange(out_weight.shape[1]) // own_width == lax.axis_index("head")
    spread = jnp.tile(residual.astype(jnp.float32), (1, out_weight.shape[1] // own_width))
    partial_value = jnp.dot(mixed, out_weight, preferred_element_type=jnp.float32)
    partial_value = partial_value + jnp.where(own_block[None, :], spread, 0.0)
    encoded = lax.psum_scatter(partial_value, "head", scatter_dimension=0, tiled=True)
    normed = (
        encoded
        * lax.rsqrt(jnp.mean(encoded * encoded, axis=1, keepdims=True) + epsilon)
        * final_gain[None, :]
    ).astype(jnp.bfloat16)
    normed = lax.all_gather(normed, "head", axis=0, tiled=True)
    key_sum = jnp.dot(normed, key_weight, preferred_element_type=jnp.float32)
    value_sum = jnp.dot(normed, value_weight, preferred_element_type=jnp.float32)
    return (key_sum.astype(jnp.bfloat16), value_sum.astype(jnp.bfloat16))


def solution(mesh):
    placed = (
        P(("groups", "seq"), "head"),
        P(("groups", "seq"), "head"),
        P(None, ("groups", "seq"), None),
        P(None, ("groups", "seq"), None),
        P(None, ("groups", "seq"), "head"),
        P("head"),
        P("head"),
        P("head"),
        P("head"),
        P("head", None),
        P(("groups", "seq"), "head"),
        P(),
        P(None, "head"),
        P(None, "head"),
    )
    return jax.shard_map(
        per_device,
        mesh=mesh,
        in_specs=placed,
        out_specs=(P(("groups", "seq"), "head"), P(("groups", "seq"), "head")),
        check_vma=False,
    )
```

```python
import jax
import jax.numpy as jnp
from jax import lax
from jax.sharding import PartitionSpec as P

STRETCH = 256
NORM_GROUPS = 4


epsilon = 1e-05
highest = lax.Precision.HIGHEST


def passed_along(value, axis, steps):
    count = lax.axis_size(axis)
    first, last = (max(0, -steps), min(count, count - steps))
    if first >= last:
        return jnp.zeros_like(value)
    return lax.ppermute(value, axis, [(source, source + steps) for source in range(first, last)])


def block_ends(acts, writes, steps, rates):
    tokens, heads, width = acts.shape
    count = tokens // STRETCH
    writes_b = writes.reshape(2, count, STRETCH, -1)
    steps_b = steps.reshape(2, count, STRETCH, heads)
    rates_b = rates.reshape(2, count, STRETCH, heads)
    position = jnp.arange(STRETCH)
    causal = jnp.stack(
        [position[:, None] >= position[None, :], position[:, None] <= position[None, :]]
    )
    cum_rate = jnp.einsum(
        "dts,dbsh->dbth", causal.astype(jnp.float32), rates_b, precision=highest
    )
    block_total = jnp.stack([cum_rate[0, :, -1], cum_rate[1, :, 0]])
    tail = jnp.exp(block_total[:, :, None, :] - cum_rate) * steps_b
    acts_b = acts.reshape(count, STRETCH, heads, width).astype(jnp.float32)
    weighted = (acts_b[None] * tail[..., None]).reshape(2, count, STRETCH, heads * width)
    ends = jnp.einsum(
        "dbsn,dbsc->dbnc", writes_b.astype(jnp.float32), weighted, precision=highest
    )
    spread = jnp.repeat(jnp.exp(block_total), width, axis=2)
    return causal, cum_rate, ends, spread


def block_within(causal, cum_rate, acts, writes, reads, steps):
    tokens, heads, width = acts.shape
    count = tokens // STRETCH
    acts_b = acts.reshape(count, STRETCH, heads, width)
    writes_b = writes.reshape(2, count, STRETCH, -1)
    reads_b = reads.reshape(2, count, STRETCH, -1)
    steps_b = steps.reshape(2, count, STRETCH, heads)
    along = jnp.transpose(cum_rate, (0, 1, 3, 2))
    spans = along[..., :, None] - along[..., None, :]
    decays = jnp.exp(jnp.where(causal[:, None, None], spans, -1e30))
    intersection = jnp.einsum(
        "dbtn,dbsn->dbts", reads_b, writes_b, preferred_element_type=jnp.float32
    )
    weights = (
        intersection[:, :, None]
        * decays
        * jnp.transpose(steps_b, (0, 1, 3, 2))[:, :, :, None, :]
    ).astype(jnp.bfloat16)
    return jnp.einsum("dbhts,bshp->dbthp", weights, acts_b, preferred_element_type=jnp.float32)


def chain_blocks(ends, decays, reverse):
    count = ends.shape[0]
    order = range(count - 1, -1, -1) if reverse else range(count)
    state = jnp.zeros_like(ends[0])
    gain = jnp.ones_like(decays[0])
    starts = [None] * count
    gains = [None] * count
    for index in order:
        starts[index] = state
        gains[index] = gain
        state = decays[index][None, :] * state + ends[index]
        gain = gain * decays[index]
    return jnp.stack(starts), jnp.stack(gains), state, gain


def relay_pair(states, gains, axis, first_round):
    count = lax.axis_size(axis)
    directions = (1, -1)
    if count <= 4:
        entering = [jnp.zeros_like(state) for state in states]
        for turn in range(count - 1):
            entering = [
                passed_along(gain[None, :] * enter + state, axis, steps)
                for enter, state, gain, steps in zip(entering, states, gains, directions)
            ]
            if turn == 0:
                entering = first_round(entering)
        if count == 1:
            entering = first_round(entering)
        return entering
    result = []
    for state, gain, steps in zip(states, gains, directions):
        distance = 1
        while distance < count:
            got_state = passed_along(state, axis, distance * steps)
            got_gain = passed_along(gain, axis, distance * steps)
            state = gain[None, :] * got_state + state
            gain = gain * got_gain
            distance *= 2
        result.append(passed_along(state, axis, steps))
    return first_round(result)


def both_directions(acts, writes, reads, steps, rates, axis):
    causal, cum_rate, ends, decays = block_ends(acts, writes, steps, rates)
    starts, gains, own_ends, own_gains = [], [], [], []
    for direction, reverse in ((0, False), (1, True)):
        start, gain, own_end, own_gain = chain_blocks(ends[direction], decays[direction], reverse)
        starts.append(start)
        gains.append(gain)
        own_ends.append(own_end)
        own_gains.append(own_gain)
    held = {}

    def first_round(entering):
        entering, held["inputs"] = lax.optimization_barrier(
            (entering, (causal, cum_rate, acts, writes, reads, steps))
        )
        return entering

    entering = relay_pair(own_ends, own_gains, axis, first_round)
    within = block_within(*held["inputs"])
    block_states = jnp.stack(
        [start + gain[:, None, :] * enter[None] for start, gain, enter in zip(starts, gains, entering)]
    )
    count = within.shape[1]
    heads, width = acts.shape[1], acts.shape[2]
    reads_b = reads.reshape(2, count, STRETCH, -1).astype(jnp.float32)
    carried = jnp.einsum("dbtn,dbnc->dbtc", reads_b, block_states, precision=highest)
    carried = carried.reshape(2, count, STRETCH, heads, width)
    outputs = within + jnp.exp(cum_rate)[..., None] * carried
    return outputs.reshape((2,) + acts.shape)


def per_device(
    inner_acts,
    gate_acts,
    write_map,
    read_map,
    step_raw,
    step_bias,
    decay_log,
    skip_gain,
    norm_gain,
    out_weight,
    residual,
    final_gain,
    key_weight,
    value_weight,
):
    tokens = inner_acts.shape[0]
    heads = step_bias.shape[0]
    width = inner_acts.shape[1] // heads
    acts = inner_acts.reshape(tokens, heads, width)
    decay_rate = -jnp.exp(decay_log)
    steps_both = jax.nn.softplus(step_raw + step_bias[None, None, :])
    outputs = both_directions(
        acts, write_map, read_map, steps_both, steps_both * decay_rate[None, None, :], "seq"
    )
    summed = outputs[0] + outputs[1] + skip_gain[None, :, None] * acts.astype(jnp.float32)
    gated = summed.reshape(tokens, heads * width) * jax.nn.silu(gate_acts.astype(jnp.float32))
    grouped = gated.reshape(tokens, NORM_GROUPS // lax.axis_size("head"), -1)
    scaled = grouped * lax.rsqrt(jnp.mean(grouped * grouped, axis=2, keepdims=True) + epsilon)
    mixed = (scaled.reshape(tokens, -1) * norm_gain[None, :]).astype(jnp.bfloat16)
    own_width = residual.shape[1]
    own_block = jnp.arange(out_weight.shape[1]) // own_width == lax.axis_index("head")
    spread = jnp.tile(residual.astype(jnp.float32), (1, out_weight.shape[1] // own_width))
    partial_value = jnp.dot(mixed, out_weight, preferred_element_type=jnp.float32)
    partial_value = partial_value + jnp.where(own_block[None, :], spread, 0.0)
    encoded = lax.psum_scatter(partial_value, "head", scatter_dimension=0, tiled=True)
    normed = (
        encoded
        * lax.rsqrt(jnp.mean(encoded * encoded, axis=1, keepdims=True) + epsilon)
        * final_gain[None, :]
    ).astype(jnp.bfloat16)
    normed = lax.all_gather(normed, "head", axis=0, tiled=True)
    key_sum = jnp.dot(normed, key_weight, preferred_element_type=jnp.float32)
    value_sum = jnp.dot(normed, value_weight, preferred_element_type=jnp.float32)
    return (key_sum.astype(jnp.bfloat16), value_sum.astype(jnp.bfloat16))


def solution(mesh):
    placed = (
        P(("groups", "seq"), "head"),
        P(("groups", "seq"), "head"),
        P(None, ("groups", "seq"), None),
        P(None, ("groups", "seq"), None),
        P(None, ("groups", "seq"), "head"),
        P("head"),
        P("head"),
        P("head"),
        P("head"),
        P("head", None),
        P(("groups", "seq"), "head"),
        P(),
        P(None, "head"),
        P(None, "head"),
    )
    return jax.shard_map(
        per_device,
        mesh=mesh,
        in_specs=placed,
        out_specs=(P(("groups", "seq"), "head"), P(("groups", "seq"), "head")),
        check_vma=False,
    )
```

```python
import jax
import jax.numpy as jnp
from jax import lax
from jax.sharding import Mesh, PartitionSpec as P

STRETCH = 256
NORM_GROUPS = 4


epsilon = 1e-05
highest = lax.Precision.HIGHEST


def passed_along(value, axis, steps):
    count = lax.axis_size(axis)
    first, last = (max(0, -steps), min(count, count - steps))
    if first >= last:
        return jnp.zeros_like(value)
    return lax.ppermute(value, axis, [(source, source + steps) for source in range(first, last)])


def block_parts(acts, writes, reads, steps, rates, reverse):
    tokens, heads, width = acts.shape
    count = tokens // STRETCH
    acts_b = acts.reshape(count, STRETCH, heads, width)
    writes_b = writes.reshape(count, STRETCH, -1)
    reads_b = reads.reshape(count, STRETCH, -1)
    steps_b = steps.reshape(count, STRETCH, heads)
    rates_b = rates.reshape(count, STRETCH, heads)
    position = jnp.arange(STRETCH)
    if reverse:
        causal = position[:, None] <= position[None, :]
    else:
        causal = position[:, None] >= position[None, :]
    cum_rate = jnp.einsum(
        "ts,bsh->bth", causal.astype(jnp.float32), rates_b, precision=highest
    )
    block_total = cum_rate[:, 0] if reverse else cum_rate[:, -1]
    along = jnp.transpose(cum_rate, (0, 2, 1))
    spans = along[:, :, :, None] - along[:, :, None, :]
    decays = jnp.exp(jnp.where(causal[None, None], spans, -1e30))
    intersection = jnp.einsum("btn,bsn->bts", reads_b, writes_b, preferred_element_type=jnp.float32)
    weights = (
        intersection[:, None] * decays * jnp.transpose(steps_b, (0, 2, 1))[:, :, None, :]
    ).astype(jnp.bfloat16)
    within = jnp.einsum("bhts,bshp->bthp", weights, acts_b, preferred_element_type=jnp.float32)
    tail = jnp.exp(block_total[:, None, :] - cum_rate) * steps_b
    weighted = acts_b.astype(jnp.float32) * tail[:, :, :, None]
    ends = jnp.einsum(
        "bshp,bsn->bhpn", weighted, writes_b.astype(jnp.float32), precision=highest
    )
    return within, cum_rate, ends, jnp.exp(block_total)


def chain_blocks(ends, decays, reverse):
    count = ends.shape[0]
    order = range(count - 1, -1, -1) if reverse else range(count)
    state = jnp.zeros_like(ends[0])
    gain = jnp.ones_like(decays[0])
    starts = [None] * count
    gains = [None] * count
    for index in order:
        starts[index] = state
        gains[index] = gain
        state = decays[index][:, None, None] * state + ends[index]
        gain = gain * decays[index]
    return jnp.stack(starts), jnp.stack(gains), state, gain


def relay(state, gain, axis, steps):
    count = lax.axis_size(axis)
    if count <= 4:
        entering = jnp.zeros_like(state)
        for _ in range(count - 1):
            entering = passed_along(gain[:, None, None] * entering + state, axis, steps)
        return entering
    distance = 1
    while distance < count:
        got_state = passed_along(state, axis, distance * steps)
        got_gain = passed_along(gain, axis, distance * steps)
        state = gain[:, None, None] * got_state + state
        gain = gain * got_gain
        distance *= 2
    return passed_along(state, axis, steps)


def direction_out(acts, writes, reads, steps, rates, reverse, axis):
    within, cum_rate, ends, decays = block_parts(acts, writes, reads, steps, rates, reverse)
    starts, gains, own_end, own_gain = chain_blocks(ends, decays, reverse)
    entering = relay(own_end, own_gain, axis, -1 if reverse else 1)
    block_states = starts + gains[:, :, None, None] * entering[None]
    count = within.shape[0]
    reads_b = reads.reshape(count, STRETCH, -1).astype(jnp.float32)
    carried = jnp.einsum("btn,bhpn->bthp", reads_b, block_states, precision=highest)
    outputs = within + jnp.exp(cum_rate)[:, :, :, None] * carried
    return outputs.reshape(acts.shape)


def swapped(value, axis):
    count = lax.axis_size(axis)
    return lax.ppermute(value, axis, [(source, count - 1 - source) for source in range(count)])


def pick(values, index):
    chosen = values[0]
    for position in range(1, len(values)):
        chosen = jnp.where(index == position, values[position], chosen)
    return chosen


def owned_rows(partial_value):
    chips, cores = lax.axis_size("head_chip"), lax.axis_size("head_core")
    chip, core = lax.axis_index("head_chip"), lax.axis_index("head_core")
    rows = partial_value.shape[0] // (chips * cores)
    blocks = partial_value.reshape(chips, cores, rows, -1)
    if cores == 2:
        keep = lax.dynamic_index_in_dim(blocks, core, axis=1, keepdims=False)
        give = lax.dynamic_index_in_dim(blocks, 1 - core, axis=1, keepdims=False)
        blocks = keep + swapped(give, "head_core")
    else:
        blocks = blocks[:, 0]
    if chips == 2:
        keep = lax.dynamic_index_in_dim(blocks, chip, axis=0, keepdims=False)
        give = lax.dynamic_index_in_dim(blocks, 1 - chip, axis=0, keepdims=False)
        return keep + swapped(give, "head_chip")
    return lax.psum_scatter(blocks, "head_chip", scatter_dimension=0, tiled=True)[0]


def all_rows(own):
    chips, cores = lax.axis_size("head_chip"), lax.axis_size("head_core")
    chip, core = lax.axis_index("head_chip"), lax.axis_index("head_core")
    if chips == 2:
        other = swapped(own, "head_chip")
        pair = pick([jnp.stack([own, other]), jnp.stack([other, own])], chip)
    else:
        pair = lax.all_gather(own, "head_chip")
    if cores == 2:
        other = swapped(pair, "head_core")
        whole = pick([jnp.stack([pair, other], axis=1), jnp.stack([other, pair], axis=1)], core)
    else:
        whole = pair[:, None]
    return whole.reshape(-1, own.shape[-1])


def per_device(
    inner_acts,
    gate_acts,
    write_map,
    read_map,
    step_raw,
    step_bias,
    decay_log,
    skip_gain,
    norm_gain,
    out_weight,
    residual,
    final_gain,
    key_weight,
    value_weight,
):
    tokens = inner_acts.shape[0]
    heads = step_bias.shape[0]
    width = inner_acts.shape[1] // heads
    acts = inner_acts.reshape(tokens, heads, width)
    decay_rate = -jnp.exp(decay_log)
    steps_fwd = jax.nn.softplus(step_raw[0] + step_bias[None, :])
    steps_bwd = jax.nn.softplus(step_raw[1] + step_bias[None, :])
    fwd_all = direction_out(
        acts, write_map[0], read_map[0], steps_fwd, steps_fwd * decay_rate[None, :], False, "seq"
    )
    bwd_all = direction_out(
        acts, write_map[1], read_map[1], steps_bwd, steps_bwd * decay_rate[None, :], True, "seq"
    )
    summed = fwd_all + bwd_all + skip_gain[None, :, None] * acts.astype(jnp.float32)
    gated = summed.reshape(tokens, heads * width) * jax.nn.silu(gate_acts.astype(jnp.float32))
    grouped = gated.reshape(tokens, NORM_GROUPS // (lax.axis_size("head_chip") * lax.axis_size("head_core")), -1)
    scaled = grouped * lax.rsqrt(jnp.mean(grouped * grouped, axis=2, keepdims=True) + epsilon)
    mixed = (scaled.reshape(tokens, -1) * norm_gain[None, :]).astype(jnp.bfloat16)
    own_width = residual.shape[1]
    own_block = jnp.arange(out_weight.shape[1]) // own_width == (lax.axis_index("head_chip") * lax.axis_size("head_core") + lax.axis_index("head_core"))
    spread = jnp.tile(residual.astype(jnp.float32), (1, out_weight.shape[1] // own_width))
    partial_value = jnp.dot(mixed, out_weight, preferred_element_type=jnp.float32)
    partial_value = partial_value + jnp.where(own_block[None, :], spread, 0.0)
    encoded = owned_rows(partial_value)
    normed = (
        encoded
        * lax.rsqrt(jnp.mean(encoded * encoded, axis=1, keepdims=True) + epsilon)
        * final_gain[None, :]
    ).astype(jnp.bfloat16)
    normed = all_rows(normed)
    key_sum = jnp.dot(normed, key_weight, preferred_element_type=jnp.float32)
    value_sum = jnp.dot(normed, value_weight, preferred_element_type=jnp.float32)
    return (key_sum.astype(jnp.bfloat16), value_sum.astype(jnp.bfloat16))


def split_head(mesh):
    shape = dict(mesh.shape)
    head = shape["head"]
    cores = 2 if head % 2 == 0 else 1
    devices = mesh.devices.reshape(shape["groups"], shape["seq"], head // cores, cores)
    return Mesh(devices, ("groups", "seq", "head_chip", "head_core"))


def solution(mesh):
    mesh = split_head(mesh)
    head = ("head_chip", "head_core")
    placed = (
        P(("groups", "seq"), head),
        P(("groups", "seq"), head),
        P(None, ("groups", "seq"), None),
        P(None, ("groups", "seq"), None),
        P(None, ("groups", "seq"), head),
        P(head),
        P(head),
        P(head),
        P(head),
        P(head, None),
        P(("groups", "seq"), head),
        P(),
        P(None, head),
        P(None, head),
    )
    return jax.shard_map(
        per_device,
        mesh=mesh,
        in_specs=placed,
        out_specs=(P(("groups", "seq"), head), P(("groups", "seq"), head)),
        check_vma=False,
    )
```

```python
import jax
import jax.numpy as jnp
from jax import lax
from jax.sharding import Mesh, PartitionSpec as P

STRETCH = 256
NORM_GROUPS = 4


epsilon = 1e-05
highest = lax.Precision.HIGHEST


def passed_along(value, axis, steps):
    count = lax.axis_size(axis)
    first, last = (max(0, -steps), min(count, count - steps))
    if first >= last:
        return jnp.zeros_like(value)
    return lax.ppermute(value, axis, [(source, source + steps) for source in range(first, last)])


def block_parts(acts, writes, reads, steps, rates, reverse):
    tokens, heads, width = acts.shape
    count = tokens // STRETCH
    acts_b = acts.reshape(count, STRETCH, heads, width)
    writes_b = writes.reshape(count, STRETCH, -1)
    reads_b = reads.reshape(count, STRETCH, -1)
    steps_b = steps.reshape(count, STRETCH, heads)
    rates_b = rates.reshape(count, STRETCH, heads)
    position = jnp.arange(STRETCH)
    if reverse:
        causal = position[:, None] <= position[None, :]
    else:
        causal = position[:, None] >= position[None, :]
    cum_rate = jnp.einsum(
        "ts,bsh->bth", causal.astype(jnp.float32), rates_b, precision=highest
    )
    block_total = cum_rate[:, 0] if reverse else cum_rate[:, -1]
    along = jnp.transpose(cum_rate, (0, 2, 1))
    spans = along[:, :, :, None] - along[:, :, None, :]
    decays = jnp.exp(jnp.where(causal[None, None], spans, -1e30))
    intersection = jnp.einsum("btn,bsn->bts", reads_b, writes_b, preferred_element_type=jnp.float32)
    weights = (
        intersection[:, None] * decays * jnp.transpose(steps_b, (0, 2, 1))[:, :, None, :]
    ).astype(jnp.bfloat16)
    within = jnp.einsum("bhts,bshp->bthp", weights, acts_b, preferred_element_type=jnp.float32)
    tail = jnp.exp(block_total[:, None, :] - cum_rate) * steps_b
    weighted = acts_b.astype(jnp.float32) * tail[:, :, :, None]
    ends = jnp.einsum(
        "bshp,bsn->bhpn", weighted, writes_b.astype(jnp.float32), precision=highest
    )
    return within, cum_rate, ends, jnp.exp(block_total)


def chain_blocks(ends, decays, reverse):
    count = ends.shape[0]
    order = range(count - 1, -1, -1) if reverse else range(count)
    state = jnp.zeros_like(ends[0])
    gain = jnp.ones_like(decays[0])
    starts = [None] * count
    gains = [None] * count
    for index in order:
        starts[index] = state
        gains[index] = gain
        state = decays[index][:, None, None] * state + ends[index]
        gain = gain * decays[index]
    return jnp.stack(starts), jnp.stack(gains), state, gain


def relay(state, gain, axis, steps):
    count = lax.axis_size(axis)
    if count <= 4:
        entering = jnp.zeros_like(state)
        for _ in range(count - 1):
            entering = passed_along(gain[:, None, None] * entering + state, axis, steps)
        return entering
    distance = 1
    while distance < count:
        got_state = passed_along(state, axis, distance * steps)
        got_gain = passed_along(gain, axis, distance * steps)
        state = gain[:, None, None] * got_state + state
        gain = gain * got_gain
        distance *= 2
    return passed_along(state, axis, steps)


def direction_out(acts, writes, reads, steps, rates, reverse, axis):
    within, cum_rate, ends, decays = block_parts(acts, writes, reads, steps, rates, reverse)
    starts, gains, own_end, own_gain = chain_blocks(ends, decays, reverse)
    entering = relay(own_end, own_gain, axis, -1 if reverse else 1)
    block_states = starts + gains[:, :, None, None] * entering[None]
    count = within.shape[0]
    reads_b = reads.reshape(count, STRETCH, -1).astype(jnp.float32)
    carried = jnp.einsum("btn,bhpn->bthp", reads_b, block_states, precision=highest)
    outputs = within + jnp.exp(cum_rate)[:, :, :, None] * carried
    return outputs.reshape(acts.shape)


def swapped(value, axis):
    count = lax.axis_size(axis)
    return lax.ppermute(value, axis, [(source, count - 1 - source) for source in range(count)])


def pick(values, index):
    chosen = values[0]
    for position in range(1, len(values)):
        chosen = jnp.where(index == position, values[position], chosen)
    return chosen


def block_at(blocks, chip, core):
    rows, width = blocks.shape[2], blocks.shape[3]
    return lax.dynamic_slice(blocks, (chip, core, 0, 0), (1, 1, rows, width))[0, 0]


def owned_rows(partial_value):
    chips, cores = lax.axis_size("head_chip"), lax.axis_size("head_core")
    if chips != 2 or cores != 2:
        return lax.psum_scatter(partial_value, ("head_chip", "head_core"), scatter_dimension=0, tiled=True)
    chip, core = lax.axis_index("head_chip"), lax.axis_index("head_core")
    blocks = partial_value.reshape(chips, cores, partial_value.shape[0] // 4, -1)
    far = block_at(blocks, 1 - chip, core) + swapped(block_at(blocks, 1 - chip, 1 - core), "head_core")
    arrived = swapped(far, "head_chip")
    near = block_at(blocks, chip, core) + swapped(block_at(blocks, chip, 1 - core), "head_core")
    return near + arrived


def project_all_rows(own, key_weight, value_weight):
    def project(rows):
        return (
            jnp.dot(rows, key_weight, preferred_element_type=jnp.float32).astype(jnp.bfloat16),
            jnp.dot(rows, value_weight, preferred_element_type=jnp.float32).astype(jnp.bfloat16),
        )

    chips, cores = lax.axis_size("head_chip"), lax.axis_size("head_core")
    if chips != 2 or cores != 2:
        return project(lax.all_gather(own, ("head_chip", "head_core"), axis=0, tiled=True))
    chip, core = lax.axis_index("head_chip"), lax.axis_index("head_core")
    other = swapped(own, "head_chip")
    partner = swapped(own, "head_core")
    partner_other = swapped(other, "head_core")
    results = [project(rows) for rows in (own, partner, other, partner_other)]
    assembled = []
    for which in range(2):
        own_p, partner_p, other_p, partner_other_p = (result[which] for result in results)
        near = pick([jnp.stack([own_p, partner_p]), jnp.stack([partner_p, own_p])], core)
        far = pick([jnp.stack([other_p, partner_other_p]), jnp.stack([partner_other_p, other_p])], core)
        whole = pick([jnp.stack([near, far]), jnp.stack([far, near])], chip)
        assembled.append(whole.reshape(-1, whole.shape[-1]))
    return tuple(assembled)


def per_device(
    inner_acts,
    gate_acts,
    write_map,
    read_map,
    step_raw,
    step_bias,
    decay_log,
    skip_gain,
    norm_gain,
    out_weight,
    residual,
    final_gain,
    key_weight,
    value_weight,
):
    tokens = inner_acts.shape[0]
    heads = step_bias.shape[0]
    width = inner_acts.shape[1] // heads
    acts = inner_acts.reshape(tokens, heads, width)
    decay_rate = -jnp.exp(decay_log)
    steps_fwd = jax.nn.softplus(step_raw[0] + step_bias[None, :])
    steps_bwd = jax.nn.softplus(step_raw[1] + step_bias[None, :])
    fwd_all = direction_out(
        acts, write_map[0], read_map[0], steps_fwd, steps_fwd * decay_rate[None, :], False, "seq"
    )
    bwd_all = direction_out(
        acts, write_map[1], read_map[1], steps_bwd, steps_bwd * decay_rate[None, :], True, "seq"
    )
    summed = fwd_all + bwd_all + skip_gain[None, :, None] * acts.astype(jnp.float32)
    gated = summed.reshape(tokens, heads * width) * jax.nn.silu(gate_acts.astype(jnp.float32))
    grouped = gated.reshape(tokens, NORM_GROUPS // (lax.axis_size("head_chip") * lax.axis_size("head_core")), -1)
    scaled = grouped * lax.rsqrt(jnp.mean(grouped * grouped, axis=2, keepdims=True) + epsilon)
    mixed = (scaled.reshape(tokens, -1) * norm_gain[None, :]).astype(jnp.bfloat16)
    own_width = residual.shape[1]
    own_block = jnp.arange(out_weight.shape[1]) // own_width == (lax.axis_index("head_chip") * lax.axis_size("head_core") + lax.axis_index("head_core"))
    spread = jnp.tile(residual.astype(jnp.float32), (1, out_weight.shape[1] // own_width))
    partial_value = jnp.dot(mixed, out_weight, preferred_element_type=jnp.float32)
    partial_value = partial_value + jnp.where(own_block[None, :], spread, 0.0)
    encoded = owned_rows(partial_value)
    normed = (
        encoded
        * lax.rsqrt(jnp.mean(encoded * encoded, axis=1, keepdims=True) + epsilon)
        * final_gain[None, :]
    ).astype(jnp.bfloat16)
    return project_all_rows(normed, key_weight, value_weight)


def split_head(mesh):
    shape = dict(mesh.shape)
    head = shape["head"]
    cores = 2 if head % 2 == 0 else 1
    devices = mesh.devices.reshape(shape["groups"], shape["seq"], head // cores, cores)
    return Mesh(devices, ("groups", "seq", "head_chip", "head_core"))


def solution(mesh):
    mesh = split_head(mesh)
    head = ("head_chip", "head_core")
    placed = (
        P(("groups", "seq"), head),
        P(("groups", "seq"), head),
        P(None, ("groups", "seq"), None),
        P(None, ("groups", "seq"), None),
        P(None, ("groups", "seq"), head),
        P(head),
        P(head),
        P(head),
        P(head),
        P(head, None),
        P(("groups", "seq"), head),
        P(),
        P(None, head),
        P(None, head),
    )
    return jax.shard_map(
        per_device,
        mesh=mesh,
        in_specs=placed,
        out_specs=(P(("groups", "seq"), head), P(("groups", "seq"), head)),
        check_vma=False,
    )
```

```python
import jax
import jax.numpy as jnp
from jax import lax
from jax.sharding import Mesh, PartitionSpec as P

STRETCH = 256
NORM_GROUPS = 4


epsilon = 1e-05
highest = lax.Precision.HIGHEST


def passed_along(value, axis, steps):
    count = lax.axis_size(axis)
    first, last = (max(0, -steps), min(count, count - steps))
    if first >= last:
        return jnp.zeros_like(value)
    return lax.ppermute(value, axis, [(source, source + steps) for source in range(first, last)])


def block_parts(acts, writes, reads, steps, rates, reverse):
    tokens, heads, width = acts.shape
    count = tokens // STRETCH
    acts_b = acts.reshape(count, STRETCH, heads, width)
    writes_b = writes.reshape(count, STRETCH, -1)
    reads_b = reads.reshape(count, STRETCH, -1)
    steps_b = steps.reshape(count, STRETCH, heads)
    rates_b = rates.reshape(count, STRETCH, heads)
    position = jnp.arange(STRETCH)
    if reverse:
        causal = position[:, None] <= position[None, :]
    else:
        causal = position[:, None] >= position[None, :]
    cum_rate = jnp.einsum(
        "ts,bsh->bth", causal.astype(jnp.float32), rates_b, precision=highest
    )
    block_total = cum_rate[:, 0] if reverse else cum_rate[:, -1]
    along = jnp.transpose(cum_rate, (0, 2, 1))
    spans = along[:, :, :, None] - along[:, :, None, :]
    decays = jnp.exp(jnp.where(causal[None, None], spans, -1e30))
    intersection = jnp.einsum("btn,bsn->bts", reads_b, writes_b, preferred_element_type=jnp.float32)
    weights = (
        intersection[:, None] * decays * jnp.transpose(steps_b, (0, 2, 1))[:, :, None, :]
    ).astype(jnp.bfloat16)
    within = jnp.einsum("bhts,bshp->bthp", weights, acts_b, preferred_element_type=jnp.float32)
    tail = jnp.exp(block_total[:, None, :] - cum_rate) * steps_b
    weighted = acts_b.astype(jnp.float32) * tail[:, :, :, None]
    ends = jnp.einsum(
        "bshp,bsn->bhpn", weighted, writes_b.astype(jnp.float32), precision=highest
    )
    return within, cum_rate, ends, jnp.exp(block_total)


def chain_blocks(ends, decays, reverse):
    count = ends.shape[0]
    order = range(count - 1, -1, -1) if reverse else range(count)
    state = jnp.zeros_like(ends[0])
    gain = jnp.ones_like(decays[0])
    starts = [None] * count
    gains = [None] * count
    for index in order:
        starts[index] = state
        gains[index] = gain
        state = decays[index][:, None, None] * state + ends[index]
        gain = gain * decays[index]
    return jnp.stack(starts), jnp.stack(gains), state, gain


def relay(state, gain, axis, steps):
    count = lax.axis_size(axis)
    if count <= 4:
        entering = jnp.zeros_like(state)
        for _ in range(count - 1):
            entering = passed_along(gain[:, None, None] * entering + state, axis, steps)
        return entering
    distance = 1
    while distance < count:
        got_state = passed_along(state, axis, distance * steps)
        got_gain = passed_along(gain, axis, distance * steps)
        state = gain[:, None, None] * got_state + state
        gain = gain * got_gain
        distance *= 2
    return passed_along(state, axis, steps)


def direction_out(acts, writes, reads, steps, rates, reverse, axis):
    within, cum_rate, ends, decays = block_parts(acts, writes, reads, steps, rates, reverse)
    starts, gains, own_end, own_gain = chain_blocks(ends, decays, reverse)
    entering = relay(own_end, own_gain, axis, -1 if reverse else 1)
    block_states = starts + gains[:, :, None, None] * entering[None]
    count = within.shape[0]
    reads_b = reads.reshape(count, STRETCH, -1).astype(jnp.float32)
    carried = jnp.einsum("btn,bhpn->bthp", reads_b, block_states, precision=highest)
    outputs = within + jnp.exp(cum_rate)[:, :, :, None] * carried
    return outputs.reshape(acts.shape)


def swapped(value, axis):
    count = lax.axis_size(axis)
    return lax.ppermute(value, axis, [(source, count - 1 - source) for source in range(count)])


def pick(values, index):
    chosen = values[0]
    for position in range(1, len(values)):
        chosen = jnp.where(index == position, values[position], chosen)
    return chosen


def block_at(blocks, chip, core):
    rows, width = blocks.shape[2], blocks.shape[3]
    return lax.dynamic_slice(blocks, (chip, core, 0, 0), (1, 1, rows, width))[0, 0]


def owned_rows(mixed, out_weight, residual):
    chips, cores = lax.axis_size("head_chip"), lax.axis_size("head_core")
    own_width = residual.shape[1]
    index = lax.axis_index("head_chip") * cores + lax.axis_index("head_core")
    own_block = jnp.arange(out_weight.shape[1]) // own_width == index
    repeats = out_weight.shape[1] // own_width

    def partial_of(rows, extra):
        value = jnp.dot(rows, out_weight, preferred_element_type=jnp.float32)
        spread = jnp.tile(extra.astype(jnp.float32), (1, repeats))
        return value + jnp.where(own_block[None, :], spread, 0.0)

    if chips != 2 or cores != 2:
        return lax.psum_scatter(
            partial_of(mixed, residual), ("head_chip", "head_core"), scatter_dimension=0, tiled=True
        )
    chip, core = lax.axis_index("head_chip"), lax.axis_index("head_core")
    rows = mixed.shape[0] // 4
    mixed4 = mixed.reshape(chips, cores, rows, -1)
    residual4 = residual.reshape(chips, cores, rows, -1)

    def part(at_chip, at_core):
        return partial_of(block_at(mixed4, at_chip, at_core), block_at(residual4, at_chip, at_core))

    far = part(1 - chip, core) + swapped(part(1 - chip, 1 - core), "head_core")
    arrived = swapped(far, "head_chip")
    near = part(chip, core) + swapped(part(chip, 1 - core), "head_core")
    return near + arrived


def project_all_rows(own, key_weight, value_weight):
    def project(rows):
        return (
            jnp.dot(rows, key_weight, preferred_element_type=jnp.float32).astype(jnp.bfloat16),
            jnp.dot(rows, value_weight, preferred_element_type=jnp.float32).astype(jnp.bfloat16),
        )

    chips, cores = lax.axis_size("head_chip"), lax.axis_size("head_core")
    if chips != 2 or cores != 2:
        return project(lax.all_gather(own, ("head_chip", "head_core"), axis=0, tiled=True))
    chip, core = lax.axis_index("head_chip"), lax.axis_index("head_core")
    other = swapped(own, "head_chip")
    partner = swapped(own, "head_core")
    partner_other = swapped(other, "head_core")
    results = [project(rows) for rows in (own, partner, other, partner_other)]
    assembled = []
    for which in range(2):
        own_p, partner_p, other_p, partner_other_p = (result[which] for result in results)
        near = pick([jnp.stack([own_p, partner_p]), jnp.stack([partner_p, own_p])], core)
        far = pick([jnp.stack([other_p, partner_other_p]), jnp.stack([partner_other_p, other_p])], core)
        whole = pick([jnp.stack([near, far]), jnp.stack([far, near])], chip)
        assembled.append(whole.reshape(-1, whole.shape[-1]))
    return tuple(assembled)


def per_device(
    inner_acts,
    gate_acts,
    write_map,
    read_map,
    step_raw,
    step_bias,
    decay_log,
    skip_gain,
    norm_gain,
    out_weight,
    residual,
    final_gain,
    key_weight,
    value_weight,
):
    tokens = inner_acts.shape[0]
    heads = step_bias.shape[0]
    width = inner_acts.shape[1] // heads
    acts = inner_acts.reshape(tokens, heads, width)
    decay_rate = -jnp.exp(decay_log)
    steps_fwd = jax.nn.softplus(step_raw[0] + step_bias[None, :])
    steps_bwd = jax.nn.softplus(step_raw[1] + step_bias[None, :])
    fwd_all = direction_out(
        acts, write_map[0], read_map[0], steps_fwd, steps_fwd * decay_rate[None, :], False, "seq"
    )
    bwd_all = direction_out(
        acts, write_map[1], read_map[1], steps_bwd, steps_bwd * decay_rate[None, :], True, "seq"
    )
    summed = fwd_all + bwd_all + skip_gain[None, :, None] * acts.astype(jnp.float32)
    gated = summed.reshape(tokens, heads * width) * jax.nn.silu(gate_acts.astype(jnp.float32))
    grouped = gated.reshape(tokens, NORM_GROUPS // (lax.axis_size("head_chip") * lax.axis_size("head_core")), -1)
    scaled = grouped * lax.rsqrt(jnp.mean(grouped * grouped, axis=2, keepdims=True) + epsilon)
    mixed = (scaled.reshape(tokens, -1) * norm_gain[None, :]).astype(jnp.bfloat16)
    encoded = owned_rows(mixed, out_weight, residual)
    normed = (
        encoded
        * lax.rsqrt(jnp.mean(encoded * encoded, axis=1, keepdims=True) + epsilon)
        * final_gain[None, :]
    ).astype(jnp.bfloat16)
    return project_all_rows(normed, key_weight, value_weight)


def split_head(mesh):
    shape = dict(mesh.shape)
    head = shape["head"]
    cores = 2 if head % 2 == 0 else 1
    devices = mesh.devices.reshape(shape["groups"], shape["seq"], head // cores, cores)
    return Mesh(devices, ("groups", "seq", "head_chip", "head_core"))


def solution(mesh):
    mesh = split_head(mesh)
    head = ("head_chip", "head_core")
    placed = (
        P(("groups", "seq"), head),
        P(("groups", "seq"), head),
        P(None, ("groups", "seq"), None),
        P(None, ("groups", "seq"), None),
        P(None, ("groups", "seq"), head),
        P(head),
        P(head),
        P(head),
        P(head),
        P(head, None),
        P(("groups", "seq"), head),
        P(),
        P(None, head),
        P(None, head),
    )
    return jax.shard_map(
        per_device,
        mesh=mesh,
        in_specs=placed,
        out_specs=(P(("groups", "seq"), head), P(("groups", "seq"), head)),
        check_vma=False,
    )
```

```python
import jax
import jax.numpy as jnp
from jax import lax
from jax.experimental.layout import Layout, with_layout_constraint
from jax.sharding import Mesh, PartitionSpec as P

STRETCH = 256
NORM_GROUPS = 4


epsilon = 1e-05
highest = lax.Precision.HIGHEST


def passed_along(value, axis, steps):
    count = lax.axis_size(axis)
    first, last = (max(0, -steps), min(count, count - steps))
    if first >= last:
        return jnp.zeros_like(value)
    return lax.ppermute(value, axis, [(source, source + steps) for source in range(first, last)])


def block_parts(acts, writes, reads, steps, rates, reverse):
    tokens, heads, width = acts.shape
    count = tokens // STRETCH
    acts_b = acts.reshape(count, STRETCH, heads, width)
    writes_b = writes.reshape(count, STRETCH, -1)
    reads_b = reads.reshape(count, STRETCH, -1)
    steps_b = steps.reshape(count, STRETCH, heads)
    rates_b = rates.reshape(count, STRETCH, heads)
    position = jnp.arange(STRETCH)
    if reverse:
        causal = position[:, None] <= position[None, :]
    else:
        causal = position[:, None] >= position[None, :]
    cum_rate = jnp.einsum(
        "ts,bsh->bth", causal.astype(jnp.float32), rates_b, precision=highest
    )
    block_total = cum_rate[:, 0] if reverse else cum_rate[:, -1]
    along = jnp.transpose(cum_rate, (0, 2, 1))
    spans = along[:, :, :, None] - along[:, :, None, :]
    decays = jnp.exp(jnp.where(causal[None, None], spans, -1e30))
    intersection = jnp.einsum("btn,bsn->bts", reads_b, writes_b, preferred_element_type=jnp.float32)
    weights = (
        intersection[:, None] * decays * jnp.transpose(steps_b, (0, 2, 1))[:, :, None, :]
    ).astype(jnp.bfloat16)
    within = jnp.einsum("bhts,bshp->bthp", weights, acts_b, preferred_element_type=jnp.float32)
    tail = jnp.exp(block_total[:, None, :] - cum_rate) * steps_b
    weighted = acts_b.astype(jnp.float32) * tail[:, :, :, None]
    ends = jnp.einsum(
        "bshp,bsn->bhpn", weighted, writes_b.astype(jnp.float32), precision=highest
    )
    return within, cum_rate, ends, jnp.exp(block_total)


def chain_blocks(ends, decays, reverse):
    count = ends.shape[0]
    order = range(count - 1, -1, -1) if reverse else range(count)
    state = jnp.zeros_like(ends[0])
    gain = jnp.ones_like(decays[0])
    starts = [None] * count
    gains = [None] * count
    for index in order:
        starts[index] = state
        gains[index] = gain
        state = decays[index][:, None, None] * state + ends[index]
        gain = gain * decays[index]
    return jnp.stack(starts), jnp.stack(gains), state, gain


def relay(state, gain, axis, steps):
    count = lax.axis_size(axis)
    if count <= 4:
        entering = jnp.zeros_like(state)
        for _ in range(count - 1):
            entering = passed_along(gain[:, None, None] * entering + state, axis, steps)
        return entering
    distance = 1
    while distance < count:
        got_state = passed_along(state, axis, distance * steps)
        got_gain = passed_along(gain, axis, distance * steps)
        state = gain[:, None, None] * got_state + state
        gain = gain * got_gain
        distance *= 2
    return passed_along(state, axis, steps)


def direction_out(acts, writes, reads, steps, rates, reverse, axis):
    within, cum_rate, ends, decays = block_parts(acts, writes, reads, steps, rates, reverse)
    starts, gains, own_end, own_gain = chain_blocks(ends, decays, reverse)
    entering = relay(own_end, own_gain, axis, -1 if reverse else 1)
    block_states = starts + gains[:, :, None, None] * entering[None]
    count = within.shape[0]
    reads_b = reads.reshape(count, STRETCH, -1).astype(jnp.float32)
    carried = jnp.einsum("btn,bhpn->bthp", reads_b, block_states, precision=highest)
    outputs = within + jnp.exp(cum_rate)[:, :, :, None] * carried
    return outputs.reshape(acts.shape)


def swapped(value, axis):
    count = lax.axis_size(axis)
    return lax.ppermute(value, axis, [(source, count - 1 - source) for source in range(count)])


def pick(values, index):
    chosen = values[0]
    for position in range(1, len(values)):
        chosen = jnp.where(index == position, values[position], chosen)
    return chosen


def block_at(blocks, chip, core):
    rows, width = blocks.shape[2], blocks.shape[3]
    return lax.dynamic_slice(blocks, (chip, core, 0, 0), (1, 1, rows, width))[0, 0]


def owned_rows(mixed, out_weight, residual):
    chips, cores = lax.axis_size("head_chip"), lax.axis_size("head_core")
    own_width = residual.shape[1]
    index = lax.axis_index("head_chip") * cores + lax.axis_index("head_core")
    own_block = jnp.arange(out_weight.shape[1]) // own_width == index
    repeats = out_weight.shape[1] // own_width

    def partial_of(rows, extra):
        value = jnp.dot(rows, out_weight, preferred_element_type=jnp.float32)
        spread = jnp.tile(extra.astype(jnp.float32), (1, repeats))
        return value + jnp.where(own_block[None, :], spread, 0.0)

    if chips != 2 or cores != 2:
        return lax.psum_scatter(
            partial_of(mixed, residual), ("head_chip", "head_core"), scatter_dimension=0, tiled=True
        )
    chip, core = lax.axis_index("head_chip"), lax.axis_index("head_core")
    rows = mixed.shape[0] // 4
    mixed4 = mixed.reshape(chips, cores, rows, -1)
    residual4 = residual.reshape(chips, cores, rows, -1)

    def part(at_chip, at_core):
        return partial_of(block_at(mixed4, at_chip, at_core), block_at(residual4, at_chip, at_core))

    far = part(1 - chip, core) + swapped(part(1 - chip, 1 - core), "head_core")
    arrived = swapped(far, "head_chip")
    near = part(chip, core) + swapped(part(chip, 1 - core), "head_core")
    return near + arrived


def project_all_rows(own, key_weight, value_weight):
    def project(rows):
        return (
            jnp.dot(rows, key_weight, preferred_element_type=jnp.float32).astype(jnp.bfloat16),
            jnp.dot(rows, value_weight, preferred_element_type=jnp.float32).astype(jnp.bfloat16),
        )

    chips, cores = lax.axis_size("head_chip"), lax.axis_size("head_core")
    if chips != 2 or cores != 2:
        return project(lax.all_gather(own, ("head_chip", "head_core"), axis=0, tiled=True))
    chip, core = lax.axis_index("head_chip"), lax.axis_index("head_core")
    other = swapped(own, "head_chip")
    partner = swapped(own, "head_core")
    partner_other = swapped(other, "head_core")
    results = [project(rows) for rows in (own, partner, other, partner_other)]
    assembled = []
    for which in range(2):
        own_p, partner_p, other_p, partner_other_p = (result[which] for result in results)
        near = pick([jnp.stack([own_p, partner_p]), jnp.stack([partner_p, own_p])], core)
        far = pick([jnp.stack([other_p, partner_other_p]), jnp.stack([partner_other_p, other_p])], core)
        whole = pick([jnp.stack([near, far]), jnp.stack([far, near])], chip)
        assembled.append(whole.reshape(-1, whole.shape[-1]))
    return tuple(assembled)


def per_device(
    inner_acts,
    gate_acts,
    write_map,
    read_map,
    step_raw,
    step_bias,
    decay_log,
    skip_gain,
    norm_gain,
    out_weight,
    residual,
    final_gain,
    key_weight,
    value_weight,
):
    tokens = inner_acts.shape[0]
    heads = step_bias.shape[0]
    width = inner_acts.shape[1] // heads
    acts = inner_acts.reshape(tokens, heads, width)
    decay_rate = -jnp.exp(decay_log)
    steps_fwd = jax.nn.softplus(step_raw[0] + step_bias[None, :])
    steps_bwd = jax.nn.softplus(step_raw[1] + step_bias[None, :])
    fwd_all = direction_out(
        acts, write_map[0], read_map[0], steps_fwd, steps_fwd * decay_rate[None, :], False, "seq"
    )
    bwd_all = direction_out(
        acts, write_map[1], read_map[1], steps_bwd, steps_bwd * decay_rate[None, :], True, "seq"
    )
    summed = fwd_all + bwd_all + skip_gain[None, :, None] * acts.astype(jnp.float32)
    summed = with_layout_constraint(summed.reshape(tokens, heads * width), Layout((0, 1)))
    gated = summed * jax.nn.silu(gate_acts.astype(jnp.float32))
    grouped = gated.reshape(tokens, NORM_GROUPS // (lax.axis_size("head_chip") * lax.axis_size("head_core")), -1)
    scaled = grouped * lax.rsqrt(jnp.mean(grouped * grouped, axis=2, keepdims=True) + epsilon)
    mixed = (scaled.reshape(tokens, -1) * norm_gain[None, :]).astype(jnp.bfloat16)
    encoded = owned_rows(mixed, out_weight, residual)
    normed = (
        encoded
        * lax.rsqrt(jnp.mean(encoded * encoded, axis=1, keepdims=True) + epsilon)
        * final_gain[None, :]
    ).astype(jnp.bfloat16)
    return project_all_rows(normed, key_weight, value_weight)


def split_head(mesh):
    shape = dict(mesh.shape)
    head = shape["head"]
    cores = 2 if head % 2 == 0 else 1
    devices = mesh.devices.reshape(shape["groups"], shape["seq"], head // cores, cores)
    return Mesh(devices, ("groups", "seq", "head_chip", "head_core"))


def solution(mesh):
    mesh = split_head(mesh)
    head = ("head_chip", "head_core")
    placed = (
        P(("groups", "seq"), head),
        P(("groups", "seq"), head),
        P(None, ("groups", "seq"), None),
        P(None, ("groups", "seq"), None),
        P(None, ("groups", "seq"), head),
        P(head),
        P(head),
        P(head),
        P(head),
        P(head, None),
        P(("groups", "seq"), head),
        P(),
        P(None, head),
        P(None, head),
    )
    return jax.shard_map(
        per_device,
        mesh=mesh,
        in_specs=placed,
        out_specs=(P(("groups", "seq"), head), P(("groups", "seq"), head)),
        check_vma=False,
    )
```

```python
import jax
import jax.numpy as jnp
from jax import lax
from jax.experimental.layout import Layout, with_layout_constraint
from jax.sharding import Mesh, PartitionSpec as P

STRETCH = 256
NORM_GROUPS = 4


epsilon = 1e-05
highest = lax.Precision.HIGHEST


def passed_along(value, axis, steps):
    count = lax.axis_size(axis)
    first, last = (max(0, -steps), min(count, count - steps))
    if first >= last:
        return jnp.zeros_like(value)
    return lax.ppermute(value, axis, [(source, source + steps) for source in range(first, last)])


def block_parts(acts, writes, reads, steps, rates, reverse):
    tokens, heads, width = acts.shape
    count = tokens // STRETCH
    acts_b = acts.reshape(count, STRETCH, heads, width)
    writes_b = writes.reshape(count, STRETCH, -1)
    reads_b = reads.reshape(count, STRETCH, -1)
    steps_b = steps.reshape(count, STRETCH, heads)
    rates_b = rates.reshape(count, STRETCH, heads)
    position = jnp.arange(STRETCH)
    if reverse:
        causal = position[:, None] <= position[None, :]
    else:
        causal = position[:, None] >= position[None, :]
    cum_rate = jnp.einsum(
        "ts,bsh->bth", causal.astype(jnp.float32), rates_b, precision=highest
    )
    block_total = cum_rate[:, 0] if reverse else cum_rate[:, -1]
    along = jnp.transpose(cum_rate, (0, 2, 1))
    spans = along[:, :, :, None] - along[:, :, None, :]
    decays = jnp.exp(jnp.where(causal[None, None], spans, -1e30))
    intersection = jnp.einsum("btn,bsn->bts", reads_b, writes_b, preferred_element_type=jnp.float32)
    weights = (
        intersection[:, None] * decays * jnp.transpose(steps_b, (0, 2, 1))[:, :, None, :]
    ).astype(jnp.bfloat16)
    within = jnp.einsum("bhts,bshp->bthp", weights, acts_b, preferred_element_type=jnp.float32)
    within = with_layout_constraint(within, Layout((0, 1, 2, 3)))
    tail = jnp.exp(block_total[:, None, :] - cum_rate) * steps_b
    weighted = acts_b.astype(jnp.float32) * tail[:, :, :, None]
    ends = jnp.einsum(
        "bshp,bsn->bhpn", weighted, writes_b.astype(jnp.float32), precision=highest
    )
    return within, cum_rate, ends, jnp.exp(block_total)


def chain_blocks(ends, decays, reverse):
    count = ends.shape[0]
    order = range(count - 1, -1, -1) if reverse else range(count)
    state = jnp.zeros_like(ends[0])
    gain = jnp.ones_like(decays[0])
    starts = [None] * count
    gains = [None] * count
    for index in order:
        starts[index] = state
        gains[index] = gain
        state = decays[index][:, None, None] * state + ends[index]
        gain = gain * decays[index]
    return jnp.stack(starts), jnp.stack(gains), state, gain


def relay(state, gain, axis, steps):
    count = lax.axis_size(axis)
    if count <= 4:
        entering = jnp.zeros_like(state)
        for _ in range(count - 1):
            entering = passed_along(gain[:, None, None] * entering + state, axis, steps)
        return entering
    distance = 1
    while distance < count:
        got_state = passed_along(state, axis, distance * steps)
        got_gain = passed_along(gain, axis, distance * steps)
        state = gain[:, None, None] * got_state + state
        gain = gain * got_gain
        distance *= 2
    return passed_along(state, axis, steps)


def direction_out(acts, writes, reads, steps, rates, reverse, axis):
    within, cum_rate, ends, decays = block_parts(acts, writes, reads, steps, rates, reverse)
    starts, gains, own_end, own_gain = chain_blocks(ends, decays, reverse)
    entering = relay(own_end, own_gain, axis, -1 if reverse else 1)
    block_states = starts + gains[:, :, None, None] * entering[None]
    count = within.shape[0]
    reads_b = reads.reshape(count, STRETCH, -1).astype(jnp.float32)
    carried = jnp.einsum("btn,bhpn->bthp", reads_b, block_states, precision=highest)
    outputs = within + jnp.exp(cum_rate)[:, :, :, None] * carried
    return outputs.reshape(acts.shape)


def swapped(value, axis):
    count = lax.axis_size(axis)
    return lax.ppermute(value, axis, [(source, count - 1 - source) for source in range(count)])


def pick(values, index):
    chosen = values[0]
    for position in range(1, len(values)):
        chosen = jnp.where(index == position, values[position], chosen)
    return chosen


def block_at(blocks, chip, core):
    rows, width = blocks.shape[2], blocks.shape[3]
    return lax.dynamic_slice(blocks, (chip, core, 0, 0), (1, 1, rows, width))[0, 0]


def owned_rows(mixed, out_weight, residual):
    chips, cores = lax.axis_size("head_chip"), lax.axis_size("head_core")
    own_width = residual.shape[1]
    index = lax.axis_index("head_chip") * cores + lax.axis_index("head_core")
    own_block = jnp.arange(out_weight.shape[1]) // own_width == index
    repeats = out_weight.shape[1] // own_width

    def partial_of(rows, extra):
        value = jnp.dot(rows, out_weight, preferred_element_type=jnp.float32)
        spread = jnp.tile(extra.astype(jnp.float32), (1, repeats))
        return value + jnp.where(own_block[None, :], spread, 0.0)

    if chips != 2 or cores != 2:
        return lax.psum_scatter(
            partial_of(mixed, residual), ("head_chip", "head_core"), scatter_dimension=0, tiled=True
        )
    chip, core = lax.axis_index("head_chip"), lax.axis_index("head_core")
    rows = mixed.shape[0] // 4
    mixed4 = mixed.reshape(chips, cores, rows, -1)
    residual4 = residual.reshape(chips, cores, rows, -1)

    def part(at_chip, at_core):
        return partial_of(block_at(mixed4, at_chip, at_core), block_at(residual4, at_chip, at_core))

    far = part(1 - chip, core) + swapped(part(1 - chip, 1 - core), "head_core")
    arrived = swapped(far, "head_chip")
    near = part(chip, core) + swapped(part(chip, 1 - core), "head_core")
    return near + arrived


def project_all_rows(own, key_weight, value_weight):
    def project(rows):
        return (
            jnp.dot(rows, key_weight, preferred_element_type=jnp.float32).astype(jnp.bfloat16),
            jnp.dot(rows, value_weight, preferred_element_type=jnp.float32).astype(jnp.bfloat16),
        )

    chips, cores = lax.axis_size("head_chip"), lax.axis_size("head_core")
    if chips != 2 or cores != 2:
        return project(lax.all_gather(own, ("head_chip", "head_core"), axis=0, tiled=True))
    chip, core = lax.axis_index("head_chip"), lax.axis_index("head_core")
    other = swapped(own, "head_chip")
    partner = swapped(own, "head_core")
    partner_other = swapped(other, "head_core")
    results = [project(rows) for rows in (own, partner, other, partner_other)]
    assembled = []
    for which in range(2):
        own_p, partner_p, other_p, partner_other_p = (result[which] for result in results)
        near = pick([jnp.stack([own_p, partner_p]), jnp.stack([partner_p, own_p])], core)
        far = pick([jnp.stack([other_p, partner_other_p]), jnp.stack([partner_other_p, other_p])], core)
        whole = pick([jnp.stack([near, far]), jnp.stack([far, near])], chip)
        assembled.append(whole.reshape(-1, whole.shape[-1]))
    return tuple(assembled)


def per_device(
    inner_acts,
    gate_acts,
    write_map,
    read_map,
    step_raw,
    step_bias,
    decay_log,
    skip_gain,
    norm_gain,
    out_weight,
    residual,
    final_gain,
    key_weight,
    value_weight,
):
    tokens = inner_acts.shape[0]
    heads = step_bias.shape[0]
    width = inner_acts.shape[1] // heads
    acts = inner_acts.reshape(tokens, heads, width)
    decay_rate = -jnp.exp(decay_log)
    steps_fwd = jax.nn.softplus(step_raw[0] + step_bias[None, :])
    steps_bwd = jax.nn.softplus(step_raw[1] + step_bias[None, :])
    fwd_all = direction_out(
        acts, write_map[0], read_map[0], steps_fwd, steps_fwd * decay_rate[None, :], False, "seq"
    )
    bwd_all = direction_out(
        acts, write_map[1], read_map[1], steps_bwd, steps_bwd * decay_rate[None, :], True, "seq"
    )
    summed = fwd_all + bwd_all + skip_gain[None, :, None] * acts.astype(jnp.float32)
    summed = with_layout_constraint(summed.reshape(tokens, heads * width), Layout((0, 1)))
    gated = summed * jax.nn.silu(gate_acts.astype(jnp.float32))
    grouped = gated.reshape(tokens, NORM_GROUPS // (lax.axis_size("head_chip") * lax.axis_size("head_core")), -1)
    scaled = grouped * lax.rsqrt(jnp.mean(grouped * grouped, axis=2, keepdims=True) + epsilon)
    mixed = (scaled.reshape(tokens, -1) * norm_gain[None, :]).astype(jnp.bfloat16)
    encoded = owned_rows(mixed, out_weight, residual)
    normed = (
        encoded
        * lax.rsqrt(jnp.mean(encoded * encoded, axis=1, keepdims=True) + epsilon)
        * final_gain[None, :]
    ).astype(jnp.bfloat16)
    return project_all_rows(normed, key_weight, value_weight)


def split_head(mesh):
    shape = dict(mesh.shape)
    head = shape["head"]
    cores = 2 if head % 2 == 0 else 1
    devices = mesh.devices.reshape(shape["groups"], shape["seq"], head // cores, cores)
    return Mesh(devices, ("groups", "seq", "head_chip", "head_core"))


def solution(mesh):
    mesh = split_head(mesh)
    head = ("head_chip", "head_core")
    placed = (
        P(("groups", "seq"), head),
        P(("groups", "seq"), head),
        P(None, ("groups", "seq"), None),
        P(None, ("groups", "seq"), None),
        P(None, ("groups", "seq"), head),
        P(head),
        P(head),
        P(head),
        P(head),
        P(head, None),
        P(("groups", "seq"), head),
        P(),
        P(None, head),
        P(None, head),
    )
    return jax.shard_map(
        per_device,
        mesh=mesh,
        in_specs=placed,
        out_specs=(P(("groups", "seq"), head), P(("groups", "seq"), head)),
        check_vma=False,
    )
```

```python
import jax
import jax.numpy as jnp
from jax import lax
from jax.experimental.layout import Layout, with_layout_constraint
from jax.sharding import Mesh, PartitionSpec as P

STRETCH = 256
NORM_GROUPS = 4


epsilon = 1e-05
highest = lax.Precision.HIGHEST


def passed_along(value, axis, steps):
    count = lax.axis_size(axis)
    first, last = (max(0, -steps), min(count, count - steps))
    if first >= last:
        return jnp.zeros_like(value)
    return lax.ppermute(value, axis, [(source, source + steps) for source in range(first, last)])


def block_parts(acts, writes, reads, steps, rates, reverse):
    tokens, heads, width = acts.shape
    count = tokens // STRETCH
    acts_b = acts.reshape(count, STRETCH, heads, width)
    writes_b = writes.reshape(count, STRETCH, -1)
    reads_b = reads.reshape(count, STRETCH, -1)
    steps_b = steps.reshape(count, STRETCH, heads)
    rates_b = rates.reshape(count, STRETCH, heads)
    position = jnp.arange(STRETCH)
    if reverse:
        causal = position[:, None] <= position[None, :]
    else:
        causal = position[:, None] >= position[None, :]
    cum_rate = jnp.einsum(
        "ts,bsh->bth", causal.astype(jnp.float32), rates_b, precision=highest
    )
    block_total = cum_rate[:, 0] if reverse else cum_rate[:, -1]
    along = jnp.transpose(cum_rate, (0, 2, 1))
    spans = along[:, :, :, None] - along[:, :, None, :]
    decays = jnp.exp(jnp.where(causal[None, None], spans, -1e30))
    intersection = jnp.einsum("btn,bsn->bts", reads_b, writes_b, preferred_element_type=jnp.float32)
    weights = (
        intersection[:, None] * decays * jnp.transpose(steps_b, (0, 2, 1))[:, :, None, :]
    ).astype(jnp.bfloat16)
    within = jnp.einsum("bhts,bshp->bthp", weights, acts_b, preferred_element_type=jnp.float32)
    tail = jnp.exp(block_total[:, None, :] - cum_rate) * steps_b
    weighted = acts_b.astype(jnp.float32) * tail[:, :, :, None]
    ends = jnp.einsum(
        "bshp,bsn->bhpn", weighted, writes_b.astype(jnp.float32), precision=highest
    )
    return within, cum_rate, ends, jnp.exp(block_total)


def chain_blocks(ends, decays, reverse):
    count = ends.shape[0]
    order = range(count - 1, -1, -1) if reverse else range(count)
    state = jnp.zeros_like(ends[0])
    gain = jnp.ones_like(decays[0])
    starts = [None] * count
    gains = [None] * count
    for index in order:
        starts[index] = state
        gains[index] = gain
        state = decays[index][:, None, None] * state + ends[index]
        gain = gain * decays[index]
    return jnp.stack(starts), jnp.stack(gains), state, gain


def relay(state, gain, axis, steps):
    count = lax.axis_size(axis)
    if count <= 4:
        entering = jnp.zeros_like(state)
        for _ in range(count - 1):
            entering = passed_along(gain[:, None, None] * entering + state, axis, steps)
        return entering
    distance = 1
    while distance < count:
        got_state = passed_along(state, axis, distance * steps)
        got_gain = passed_along(gain, axis, distance * steps)
        state = gain[:, None, None] * got_state + state
        gain = gain * got_gain
        distance *= 2
    return passed_along(state, axis, steps)


def direction_out(acts, writes, reads, steps, rates, reverse, axis):
    within, cum_rate, ends, decays = block_parts(acts, writes, reads, steps, rates, reverse)
    starts, gains, own_end, own_gain = chain_blocks(ends, decays, reverse)
    entering = relay(own_end, own_gain, axis, -1 if reverse else 1)
    block_states = starts + gains[:, :, None, None] * entering[None]
    count = within.shape[0]
    reads_b = reads.reshape(count, STRETCH, -1).astype(jnp.float32)
    carried = jnp.einsum("btn,bhpn->bthp", reads_b, block_states, precision=highest)
    outputs = within + jnp.exp(cum_rate)[:, :, :, None] * carried
    return outputs.reshape(acts.shape)


def swapped(value, axis):
    count = lax.axis_size(axis)
    return lax.ppermute(value, axis, [(source, count - 1 - source) for source in range(count)])


def pick(values, index):
    chosen = values[0]
    for position in range(1, len(values)):
        chosen = jnp.where(index == position, values[position], chosen)
    return chosen


def block_at(blocks, chip, core):
    rows, width = blocks.shape[2], blocks.shape[3]
    return lax.dynamic_slice(blocks, (chip, core, 0, 0), (1, 1, rows, width))[0, 0]


def owned_rows(mixed, out_weight, residual):
    chips, cores = lax.axis_size("head_chip"), lax.axis_size("head_core")
    own_width = residual.shape[1]
    index = lax.axis_index("head_chip") * cores + lax.axis_index("head_core")
    own_block = jnp.arange(out_weight.shape[1]) // own_width == index
    repeats = out_weight.shape[1] // own_width

    def partial_of(rows, extra):
        value = jnp.dot(rows, out_weight, preferred_element_type=jnp.float32)
        spread = jnp.tile(extra.astype(jnp.float32), (1, repeats))
        return value + jnp.where(own_block[None, :], spread, 0.0)

    if chips != 2 or cores != 2:
        return lax.psum_scatter(
            partial_of(mixed, residual), ("head_chip", "head_core"), scatter_dimension=0, tiled=True
        )
    chip, core = lax.axis_index("head_chip"), lax.axis_index("head_core")
    rows = mixed.shape[0] // 4
    mixed4 = mixed.reshape(chips, cores, rows, -1)
    residual4 = residual.reshape(chips, cores, rows, -1)

    def part(at_chip, at_core):
        return partial_of(block_at(mixed4, at_chip, at_core), block_at(residual4, at_chip, at_core))

    far = part(1 - chip, core) + swapped(part(1 - chip, 1 - core), "head_core")
    far, (mixed4, residual4) = lax.optimization_barrier((far, (mixed4, residual4)))
    arrived = swapped(far, "head_chip")
    near = part(chip, core) + swapped(part(chip, 1 - core), "head_core")
    return near + arrived


def project_all_rows(own, key_weight, value_weight):
    def project(rows):
        return (
            jnp.dot(rows, key_weight, preferred_element_type=jnp.float32).astype(jnp.bfloat16),
            jnp.dot(rows, value_weight, preferred_element_type=jnp.float32).astype(jnp.bfloat16),
        )

    chips, cores = lax.axis_size("head_chip"), lax.axis_size("head_core")
    if chips != 2 or cores != 2:
        return project(lax.all_gather(own, ("head_chip", "head_core"), axis=0, tiled=True))
    chip, core = lax.axis_index("head_chip"), lax.axis_index("head_core")
    other = swapped(own, "head_chip")
    partner = swapped(own, "head_core")
    partner_other = swapped(other, "head_core")
    results = [project(rows) for rows in (own, partner, other, partner_other)]
    assembled = []
    for which in range(2):
        own_p, partner_p, other_p, partner_other_p = (result[which] for result in results)
        near = pick([jnp.stack([own_p, partner_p]), jnp.stack([partner_p, own_p])], core)
        far = pick([jnp.stack([other_p, partner_other_p]), jnp.stack([partner_other_p, other_p])], core)
        whole = pick([jnp.stack([near, far]), jnp.stack([far, near])], chip)
        assembled.append(whole.reshape(-1, whole.shape[-1]))
    return tuple(assembled)


def per_device(
    inner_acts,
    gate_acts,
    write_map,
    read_map,
    step_raw,
    step_bias,
    decay_log,
    skip_gain,
    norm_gain,
    out_weight,
    residual,
    final_gain,
    key_weight,
    value_weight,
):
    tokens = inner_acts.shape[0]
    heads = step_bias.shape[0]
    width = inner_acts.shape[1] // heads
    acts = inner_acts.reshape(tokens, heads, width)
    decay_rate = -jnp.exp(decay_log)
    steps_fwd = jax.nn.softplus(step_raw[0] + step_bias[None, :])
    steps_bwd = jax.nn.softplus(step_raw[1] + step_bias[None, :])
    fwd_all = direction_out(
        acts, write_map[0], read_map[0], steps_fwd, steps_fwd * decay_rate[None, :], False, "seq"
    )
    bwd_all = direction_out(
        acts, write_map[1], read_map[1], steps_bwd, steps_bwd * decay_rate[None, :], True, "seq"
    )
    summed = fwd_all + bwd_all + skip_gain[None, :, None] * acts.astype(jnp.float32)
    summed = with_layout_constraint(summed.reshape(tokens, heads * width), Layout((0, 1)))
    gated = summed * jax.nn.silu(gate_acts.astype(jnp.float32))
    grouped = gated.reshape(tokens, NORM_GROUPS // (lax.axis_size("head_chip") * lax.axis_size("head_core")), -1)
    scaled = grouped * lax.rsqrt(jnp.mean(grouped * grouped, axis=2, keepdims=True) + epsilon)
    mixed = (scaled.reshape(tokens, -1) * norm_gain[None, :]).astype(jnp.bfloat16)
    encoded = owned_rows(mixed, out_weight, residual)
    normed = (
        encoded
        * lax.rsqrt(jnp.mean(encoded * encoded, axis=1, keepdims=True) + epsilon)
        * final_gain[None, :]
    ).astype(jnp.bfloat16)
    return project_all_rows(normed, key_weight, value_weight)


def split_head(mesh):
    shape = dict(mesh.shape)
    head = shape["head"]
    cores = 2 if head % 2 == 0 else 1
    devices = mesh.devices.reshape(shape["groups"], shape["seq"], head // cores, cores)
    return Mesh(devices, ("groups", "seq", "head_chip", "head_core"))


def solution(mesh):
    mesh = split_head(mesh)
    head = ("head_chip", "head_core")
    placed = (
        P(("groups", "seq"), head),
        P(("groups", "seq"), head),
        P(None, ("groups", "seq"), None),
        P(None, ("groups", "seq"), None),
        P(None, ("groups", "seq"), head),
        P(head),
        P(head),
        P(head),
        P(head),
        P(head, None),
        P(("groups", "seq"), head),
        P(),
        P(None, head),
        P(None, head),
    )
    return jax.shard_map(
        per_device,
        mesh=mesh,
        in_specs=placed,
        out_specs=(P(("groups", "seq"), head), P(("groups", "seq"), head)),
        check_vma=False,
    )
```

```python
import jax
import jax.numpy as jnp
from jax import lax
from jax.experimental.layout import Layout, with_layout_constraint
from jax.sharding import Mesh, PartitionSpec as P

STRETCH = 256
NORM_GROUPS = 4


epsilon = 1e-05
highest = lax.Precision.HIGHEST
high = lax.Precision.HIGH


def passed_along(value, axis, steps):
    count = lax.axis_size(axis)
    first, last = (max(0, -steps), min(count, count - steps))
    if first >= last:
        return jnp.zeros_like(value)
    return lax.ppermute(value, axis, [(source, source + steps) for source in range(first, last)])


def block_parts(acts, writes, reads, steps, rates, reverse):
    tokens, heads, width = acts.shape
    count = tokens // STRETCH
    acts_b = acts.reshape(count, STRETCH, heads, width)
    writes_b = writes.reshape(count, STRETCH, -1)
    reads_b = reads.reshape(count, STRETCH, -1)
    steps_b = steps.reshape(count, STRETCH, heads)
    rates_b = rates.reshape(count, STRETCH, heads)
    position = jnp.arange(STRETCH)
    if reverse:
        causal = position[:, None] <= position[None, :]
    else:
        causal = position[:, None] >= position[None, :]
    cum_rate = jnp.einsum(
        "ts,bsh->bth", causal.astype(jnp.float32), rates_b, precision=highest
    )
    block_total = cum_rate[:, 0] if reverse else cum_rate[:, -1]
    along = jnp.transpose(cum_rate, (0, 2, 1))
    spans = along[:, :, :, None] - along[:, :, None, :]
    decays = jnp.exp(jnp.where(causal[None, None], spans, -1e30))
    intersection = jnp.einsum("btn,bsn->bts", reads_b, writes_b, preferred_element_type=jnp.float32)
    weights = (
        intersection[:, None] * decays * jnp.transpose(steps_b, (0, 2, 1))[:, :, None, :]
    ).astype(jnp.bfloat16)
    within = jnp.einsum("bhts,bshp->bthp", weights, acts_b, preferred_element_type=jnp.float32)
    tail = jnp.exp(block_total[:, None, :] - cum_rate) * steps_b
    weighted = acts_b.astype(jnp.float32) * tail[:, :, :, None]
    ends = jnp.einsum(
        "bshp,bsn->bhpn", weighted, writes_b.astype(jnp.float32), precision=high
    )
    return within, cum_rate, ends, jnp.exp(block_total)


def chain_blocks(ends, decays, reverse):
    count = ends.shape[0]
    order = range(count - 1, -1, -1) if reverse else range(count)
    state = jnp.zeros_like(ends[0])
    gain = jnp.ones_like(decays[0])
    starts = [None] * count
    gains = [None] * count
    for index in order:
        starts[index] = state
        gains[index] = gain
        state = decays[index][:, None, None] * state + ends[index]
        gain = gain * decays[index]
    return jnp.stack(starts), jnp.stack(gains), state, gain


def relay(state, gain, axis, steps):
    count = lax.axis_size(axis)
    if count <= 4:
        entering = jnp.zeros_like(state)
        for _ in range(count - 1):
            entering = passed_along(gain[:, None, None] * entering + state, axis, steps)
        return entering
    distance = 1
    while distance < count:
        got_state = passed_along(state, axis, distance * steps)
        got_gain = passed_along(gain, axis, distance * steps)
        state = gain[:, None, None] * got_state + state
        gain = gain * got_gain
        distance *= 2
    return passed_along(state, axis, steps)


def direction_out(acts, writes, reads, steps, rates, reverse, axis):
    within, cum_rate, ends, decays = block_parts(acts, writes, reads, steps, rates, reverse)
    starts, gains, own_end, own_gain = chain_blocks(ends, decays, reverse)
    entering = relay(own_end, own_gain, axis, -1 if reverse else 1)
    block_states = starts + gains[:, :, None, None] * entering[None]
    count = within.shape[0]
    reads_b = reads.reshape(count, STRETCH, -1).astype(jnp.float32)
    carried = jnp.einsum("btn,bhpn->bthp", reads_b, block_states, precision=high)
    outputs = within + jnp.exp(cum_rate)[:, :, :, None] * carried
    return outputs.reshape(acts.shape)


def swapped(value, axis):
    count = lax.axis_size(axis)
    return lax.ppermute(value, axis, [(source, count - 1 - source) for source in range(count)])


def pick(values, index):
    chosen = values[0]
    for position in range(1, len(values)):
        chosen = jnp.where(index == position, values[position], chosen)
    return chosen


def block_at(blocks, chip, core):
    rows, width = blocks.shape[2], blocks.shape[3]
    return lax.dynamic_slice(blocks, (chip, core, 0, 0), (1, 1, rows, width))[0, 0]


def owned_rows(mixed, out_weight, residual):
    chips, cores = lax.axis_size("head_chip"), lax.axis_size("head_core")
    own_width = residual.shape[1]
    index = lax.axis_index("head_chip") * cores + lax.axis_index("head_core")
    own_block = jnp.arange(out_weight.shape[1]) // own_width == index
    repeats = out_weight.shape[1] // own_width

    def partial_of(rows, extra):
        value = jnp.dot(rows, out_weight, preferred_element_type=jnp.float32)
        spread = jnp.tile(extra.astype(jnp.float32), (1, repeats))
        return value + jnp.where(own_block[None, :], spread, 0.0)

    if chips != 2 or cores != 2:
        return lax.psum_scatter(
            partial_of(mixed, residual), ("head_chip", "head_core"), scatter_dimension=0, tiled=True
        )
    chip, core = lax.axis_index("head_chip"), lax.axis_index("head_core")
    rows = mixed.shape[0] // 4
    mixed4 = mixed.reshape(chips, cores, rows, -1)
    residual4 = residual.reshape(chips, cores, rows, -1)

    def part(at_chip, at_core):
        return partial_of(block_at(mixed4, at_chip, at_core), block_at(residual4, at_chip, at_core))

    far = part(1 - chip, core) + swapped(part(1 - chip, 1 - core), "head_core")
    arrived = swapped(far, "head_chip")
    near = part(chip, core) + swapped(part(chip, 1 - core), "head_core")
    return near + arrived


def project_all_rows(own, key_weight, value_weight):
    def project(rows):
        return (
            jnp.dot(rows, key_weight, preferred_element_type=jnp.float32).astype(jnp.bfloat16),
            jnp.dot(rows, value_weight, preferred_element_type=jnp.float32).astype(jnp.bfloat16),
        )

    chips, cores = lax.axis_size("head_chip"), lax.axis_size("head_core")
    if chips != 2 or cores != 2:
        return project(lax.all_gather(own, ("head_chip", "head_core"), axis=0, tiled=True))
    chip, core = lax.axis_index("head_chip"), lax.axis_index("head_core")
    other = swapped(own, "head_chip")
    partner = swapped(own, "head_core")
    partner_other = swapped(other, "head_core")
    results = [project(rows) for rows in (own, partner, other, partner_other)]
    assembled = []
    for which in range(2):
        own_p, partner_p, other_p, partner_other_p = (result[which] for result in results)
        near = pick([jnp.stack([own_p, partner_p]), jnp.stack([partner_p, own_p])], core)
        far = pick([jnp.stack([other_p, partner_other_p]), jnp.stack([partner_other_p, other_p])], core)
        whole = pick([jnp.stack([near, far]), jnp.stack([far, near])], chip)
        assembled.append(whole.reshape(-1, whole.shape[-1]))
    return tuple(assembled)


def per_device(
    inner_acts,
    gate_acts,
    write_map,
    read_map,
    step_raw,
    step_bias,
    decay_log,
    skip_gain,
    norm_gain,
    out_weight,
    residual,
    final_gain,
    key_weight,
    value_weight,
):
    tokens = inner_acts.shape[0]
    heads = step_bias.shape[0]
    width = inner_acts.shape[1] // heads
    acts = inner_acts.reshape(tokens, heads, width)
    decay_rate = -jnp.exp(decay_log)
    steps_fwd = jax.nn.softplus(step_raw[0] + step_bias[None, :])
    steps_bwd = jax.nn.softplus(step_raw[1] + step_bias[None, :])
    fwd_all = direction_out(
        acts, write_map[0], read_map[0], steps_fwd, steps_fwd * decay_rate[None, :], False, "seq"
    )
    bwd_all = direction_out(
        acts, write_map[1], read_map[1], steps_bwd, steps_bwd * decay_rate[None, :], True, "seq"
    )
    summed = fwd_all + bwd_all + skip_gain[None, :, None] * acts.astype(jnp.float32)
    summed = with_layout_constraint(summed.reshape(tokens, heads * width), Layout((0, 1)))
    gated = summed * jax.nn.silu(gate_acts.astype(jnp.float32))
    grouped = gated.reshape(tokens, NORM_GROUPS // (lax.axis_size("head_chip") * lax.axis_size("head_core")), -1)
    scaled = grouped * lax.rsqrt(jnp.mean(grouped * grouped, axis=2, keepdims=True) + epsilon)
    mixed = (scaled.reshape(tokens, -1) * norm_gain[None, :]).astype(jnp.bfloat16)
    encoded = owned_rows(mixed, out_weight, residual)
    normed = (
        encoded
        * lax.rsqrt(jnp.mean(encoded * encoded, axis=1, keepdims=True) + epsilon)
        * final_gain[None, :]
    ).astype(jnp.bfloat16)
    return project_all_rows(normed, key_weight, value_weight)


def split_head(mesh):
    shape = dict(mesh.shape)
    head = shape["head"]
    cores = 2 if head % 2 == 0 else 1
    devices = mesh.devices.reshape(shape["groups"], shape["seq"], head // cores, cores)
    return Mesh(devices, ("groups", "seq", "head_chip", "head_core"))


def solution(mesh):
    mesh = split_head(mesh)
    head = ("head_chip", "head_core")
    placed = (
        P(("groups", "seq"), head),
        P(("groups", "seq"), head),
        P(None, ("groups", "seq"), None),
        P(None, ("groups", "seq"), None),
        P(None, ("groups", "seq"), head),
        P(head),
        P(head),
        P(head),
        P(head),
        P(head, None),
        P(("groups", "seq"), head),
        P(),
        P(None, head),
        P(None, head),
    )
    return jax.shard_map(
        per_device,
        mesh=mesh,
        in_specs=placed,
        out_specs=(P(("groups", "seq"), head), P(("groups", "seq"), head)),
        check_vma=False,
    )
```

```python
import jax
import jax.numpy as jnp
from jax import lax
from jax.experimental.layout import Layout, with_layout_constraint
from jax.sharding import Mesh, PartitionSpec as P

STRETCH = 256
NORM_GROUPS = 4


epsilon = 1e-05
highest = lax.Precision.HIGHEST


def passed_along(value, axis, steps):
    count = lax.axis_size(axis)
    first, last = (max(0, -steps), min(count, count - steps))
    if first >= last:
        return jnp.zeros_like(value)
    return lax.ppermute(value, axis, [(source, source + steps) for source in range(first, last)])


def block_parts(acts, writes, reads, steps, rates, reverse):
    tokens, heads, width = acts.shape
    count = tokens // STRETCH
    acts_b = acts.reshape(count, STRETCH, heads, width)
    writes_b = writes.reshape(count, STRETCH, -1)
    reads_b = reads.reshape(count, STRETCH, -1)
    steps_b = steps.reshape(count, STRETCH, heads)
    rates_b = rates.reshape(count, STRETCH, heads)
    position = jnp.arange(STRETCH)
    if reverse:
        causal = position[:, None] <= position[None, :]
    else:
        causal = position[:, None] >= position[None, :]
    cum_rate = jnp.einsum(
        "ts,bsh->bth", causal.astype(jnp.float32), rates_b, precision=highest
    )
    block_total = cum_rate[:, 0] if reverse else cum_rate[:, -1]
    along = jnp.transpose(cum_rate, (0, 2, 1))
    spans = along[:, :, :, None] - along[:, :, None, :]
    decays = jnp.exp(jnp.where(causal[None, None], spans, -1e30))
    intersection = jnp.einsum("btn,bsn->bts", reads_b, writes_b, preferred_element_type=jnp.float32)
    weights = (
        intersection[:, None] * decays * jnp.transpose(steps_b, (0, 2, 1))[:, :, None, :]
    ).astype(jnp.bfloat16)
    within = jnp.einsum("bhts,bshp->bthp", weights, acts_b, preferred_element_type=jnp.float32)
    tail = jnp.exp(block_total[:, None, :] - cum_rate) * steps_b
    weighted = acts_b.astype(jnp.float32) * tail[:, :, :, None]
    ends = jnp.einsum(
        "bshp,bsn->bhpn", weighted, writes_b.astype(jnp.float32), precision=highest
    )
    return within, cum_rate, ends, jnp.exp(block_total)


def chain_blocks(ends, decays, reverse):
    count = ends.shape[0]
    order = range(count - 1, -1, -1) if reverse else range(count)
    state = jnp.zeros_like(ends[0])
    gain = jnp.ones_like(decays[0])
    starts = [None] * count
    gains = [None] * count
    for index in order:
        starts[index] = state
        gains[index] = gain
        state = decays[index][:, None, None] * state + ends[index]
        gain = gain * decays[index]
    return jnp.stack(starts), jnp.stack(gains), state, gain


def relay(state, gain, axis, steps):
    count = lax.axis_size(axis)
    if count <= 4:
        entering = jnp.zeros_like(state)
        for _ in range(count - 1):
            entering = passed_along(gain[:, None, None] * entering + state, axis, steps)
        return entering
    distance = 1
    while distance < count:
        got_state = passed_along(state, axis, distance * steps)
        got_gain = passed_along(gain, axis, distance * steps)
        state = gain[:, None, None] * got_state + state
        gain = gain * got_gain
        distance *= 2
    return passed_along(state, axis, steps)


def direction_out(acts, writes, reads, steps, rates, reverse, axis):
    within, cum_rate, ends, decays = block_parts(acts, writes, reads, steps, rates, reverse)
    starts, gains, own_end, own_gain = chain_blocks(ends, decays, reverse)
    entering = relay(own_end, own_gain, axis, -1 if reverse else 1)
    block_states = starts + gains[:, :, None, None] * entering[None]
    count = within.shape[0]
    reads_b = reads.reshape(count, STRETCH, -1).astype(jnp.float32)
    carried = jnp.einsum("btn,bhpn->bthp", reads_b, block_states, precision=highest)
    outputs = within + jnp.exp(cum_rate)[:, :, :, None] * carried
    return outputs.reshape(acts.shape)


def swapped(value, axis):
    count = lax.axis_size(axis)
    return lax.ppermute(value, axis, [(source, count - 1 - source) for source in range(count)])


def pick(values, index):
    chosen = values[0]
    for position in range(1, len(values)):
        chosen = jnp.where(index == position, values[position], chosen)
    return chosen


def block_at(blocks, chip, core):
    rows, width = blocks.shape[2], blocks.shape[3]
    return lax.dynamic_slice(blocks, (chip, core, 0, 0), (1, 1, rows, width))[0, 0]


def owned_rows(mixed, out_weight, residual):
    chips, cores = lax.axis_size("head_chip"), lax.axis_size("head_core")
    own_width = residual.shape[1]
    index = lax.axis_index("head_chip") * cores + lax.axis_index("head_core")
    own_block = jnp.arange(out_weight.shape[1]) // own_width == index
    repeats = out_weight.shape[1] // own_width

    def partial_of(rows, extra):
        value = jnp.dot(rows, out_weight, preferred_element_type=jnp.float32)
        spread = jnp.tile(extra.astype(jnp.float32), (1, repeats))
        return value + jnp.where(own_block[None, :], spread, 0.0)

    if chips != 2 or cores != 2:
        return lax.psum_scatter(
            partial_of(mixed, residual), ("head_chip", "head_core"), scatter_dimension=0, tiled=True
        )
    chip, core = lax.axis_index("head_chip"), lax.axis_index("head_core")
    rows = mixed.shape[0] // 4
    mixed4 = mixed.reshape(chips, cores, rows, -1)
    residual4 = residual.reshape(chips, cores, rows, -1)

    def part(at_chip, at_core):
        return partial_of(block_at(mixed4, at_chip, at_core), block_at(residual4, at_chip, at_core))

    far = part(1 - chip, core) + swapped(part(1 - chip, 1 - core), "head_core")
    arrived = swapped(far, "head_chip")
    near = part(chip, core) + swapped(part(chip, 1 - core), "head_core")
    return near + arrived


def project_all_rows(own, key_weight, value_weight):
    def project(rows):
        return (
            jnp.dot(rows, key_weight, preferred_element_type=jnp.float32).astype(jnp.bfloat16),
            jnp.dot(rows, value_weight, preferred_element_type=jnp.float32).astype(jnp.bfloat16),
        )

    chips, cores = lax.axis_size("head_chip"), lax.axis_size("head_core")
    if chips != 2 or cores != 2:
        return project(lax.all_gather(own, ("head_chip", "head_core"), axis=0, tiled=True))
    chip, core = lax.axis_index("head_chip"), lax.axis_index("head_core")
    other = swapped(own, "head_chip")
    partner = swapped(own, "head_core")
    partner_other = swapped(other, "head_core")
    results = [project(rows) for rows in (own, partner, other, partner_other)]
    assembled = []
    for which in range(2):
        own_p, partner_p, other_p, partner_other_p = (result[which] for result in results)
        near = pick([jnp.stack([own_p, partner_p]), jnp.stack([partner_p, own_p])], core)
        far = pick([jnp.stack([other_p, partner_other_p]), jnp.stack([partner_other_p, other_p])], core)
        whole = pick([jnp.stack([near, far]), jnp.stack([far, near])], chip)
        assembled.append(whole.reshape(-1, whole.shape[-1]))
    return tuple(assembled)


def per_device(
    inner_acts,
    gate_acts,
    write_map,
    read_map,
    step_raw,
    step_bias,
    decay_log,
    skip_gain,
    norm_gain,
    out_weight,
    residual,
    final_gain,
    key_weight,
    value_weight,
):
    tokens = inner_acts.shape[0]
    heads = step_bias.shape[0]
    width = inner_acts.shape[1] // heads
    acts = inner_acts.reshape(tokens, heads, width)
    decay_rate = -jnp.exp(decay_log)
    steps_fwd = jax.nn.softplus(step_raw[0] + step_bias[None, :])
    steps_bwd = jax.nn.softplus(step_raw[1] + step_bias[None, :])
    fwd_all = direction_out(
        acts, write_map[0], read_map[0], steps_fwd, steps_fwd * decay_rate[None, :], False, "seq"
    )
    bwd_all = direction_out(
        acts, write_map[1], read_map[1], steps_bwd, steps_bwd * decay_rate[None, :], True, "seq"
    )
    summed = fwd_all + bwd_all + skip_gain[None, :, None] * acts.astype(jnp.float32)
    summed = with_layout_constraint(summed.reshape(tokens, heads * width), Layout((0, 1)))
    gated = summed * jax.nn.silu(gate_acts.astype(jnp.float32))
    grouped = gated.reshape(tokens, NORM_GROUPS // (lax.axis_size("head_chip") * lax.axis_size("head_core")), -1)
    squares = jnp.einsum(
        "tgc,c->tg", grouped * grouped, jnp.ones((grouped.shape[2],), jnp.float32), precision=highest
    )
    scaled = grouped * lax.rsqrt(squares[:, :, None] / grouped.shape[2] + epsilon)
    mixed = (scaled.reshape(tokens, -1) * norm_gain[None, :]).astype(jnp.bfloat16)
    encoded = owned_rows(mixed, out_weight, residual)
    normed = (
        encoded
        * lax.rsqrt(jnp.mean(encoded * encoded, axis=1, keepdims=True) + epsilon)
        * final_gain[None, :]
    ).astype(jnp.bfloat16)
    return project_all_rows(normed, key_weight, value_weight)


def split_head(mesh):
    shape = dict(mesh.shape)
    head = shape["head"]
    cores = 2 if head % 2 == 0 else 1
    devices = mesh.devices.reshape(shape["groups"], shape["seq"], head // cores, cores)
    return Mesh(devices, ("groups", "seq", "head_chip", "head_core"))


def solution(mesh):
    mesh = split_head(mesh)
    head = ("head_chip", "head_core")
    placed = (
        P(("groups", "seq"), head),
        P(("groups", "seq"), head),
        P(None, ("groups", "seq"), None),
        P(None, ("groups", "seq"), None),
        P(None, ("groups", "seq"), head),
        P(head),
        P(head),
        P(head),
        P(head),
        P(head, None),
        P(("groups", "seq"), head),
        P(),
        P(None, head),
        P(None, head),
    )
    return jax.shard_map(
        per_device,
        mesh=mesh,
        in_specs=placed,
        out_specs=(P(("groups", "seq"), head), P(("groups", "seq"), head)),
        check_vma=False,
    )
```

```python
import jax
import jax.numpy as jnp
from jax import lax
from jax.experimental.layout import Layout, with_layout_constraint
from jax.sharding import Mesh, PartitionSpec as P

STRETCH = 256
NORM_GROUPS = 4


epsilon = 1e-05
highest = lax.Precision.HIGHEST


def passed_along(value, axis, steps):
    count = lax.axis_size(axis)
    first, last = (max(0, -steps), min(count, count - steps))
    if first >= last:
        return jnp.zeros_like(value)
    return lax.ppermute(value, axis, [(source, source + steps) for source in range(first, last)])


def block_parts(acts, writes, reads, steps, rates, reverse):
    tokens, heads, width = acts.shape
    count = tokens // STRETCH
    acts_b = acts.reshape(count, STRETCH, heads, width)
    writes_b = writes.reshape(count, STRETCH, -1)
    reads_b = reads.reshape(count, STRETCH, -1)
    steps_b = steps.reshape(count, STRETCH, heads)
    rates_b = rates.reshape(count, STRETCH, heads)
    position = jnp.arange(STRETCH)
    if reverse:
        causal = position[:, None] <= position[None, :]
    else:
        causal = position[:, None] >= position[None, :]
    cum_rate = jnp.einsum(
        "ts,bsh->bth", causal.astype(jnp.float32), rates_b, precision=highest
    )
    block_total = cum_rate[:, 0] if reverse else cum_rate[:, -1]
    along = jnp.transpose(cum_rate, (0, 2, 1))
    spans = along[:, :, :, None] - along[:, :, None, :]
    decays = jnp.exp(jnp.where(causal[None, None], spans, -1e30))
    intersection = jnp.einsum("btn,bsn->bts", reads_b, writes_b, preferred_element_type=jnp.float32)
    weights = (
        intersection[:, None] * decays * jnp.transpose(steps_b, (0, 2, 1))[:, :, None, :]
    ).astype(jnp.bfloat16)
    within = jnp.einsum("bhts,bshp->bthp", weights, acts_b, preferred_element_type=jnp.float32)
    tail = jnp.exp(block_total[:, None, :] - cum_rate) * steps_b
    weighted = acts_b.astype(jnp.float32) * tail[:, :, :, None]
    ends = jnp.einsum(
        "bshp,bsn->bhpn", weighted, writes_b.astype(jnp.float32), precision=highest
    )
    return within, cum_rate, ends, jnp.exp(block_total)


def chain_blocks(ends, decays, reverse):
    count = ends.shape[0]
    order = range(count - 1, -1, -1) if reverse else range(count)
    state = jnp.zeros_like(ends[0])
    gain = jnp.ones_like(decays[0])
    starts = [None] * count
    gains = [None] * count
    for index in order:
        starts[index] = state
        gains[index] = gain
        state = decays[index][:, None, None] * state + ends[index]
        gain = gain * decays[index]
    return jnp.stack(starts), jnp.stack(gains), state, gain


def relay(state, gain, axis, steps):
    count = lax.axis_size(axis)
    if count <= 4:
        entering = jnp.zeros_like(state)
        for turn in range(count - 1):
            leaving = state if turn == 0 else gain[:, None, None] * entering + state
            entering = passed_along(leaving, axis, steps)
        return entering
    distance = 1
    while distance < count:
        got_state = passed_along(state, axis, distance * steps)
        got_gain = passed_along(gain, axis, distance * steps)
        state = gain[:, None, None] * got_state + state
        gain = gain * got_gain
        distance *= 2
    return passed_along(state, axis, steps)


def direction_out(acts, writes, reads, steps, rates, reverse, axis):
    within, cum_rate, ends, decays = block_parts(acts, writes, reads, steps, rates, reverse)
    starts, gains, own_end, own_gain = chain_blocks(ends, decays, reverse)
    entering = relay(own_end, own_gain, axis, -1 if reverse else 1)
    block_states = starts + gains[:, :, None, None] * entering[None]
    count = within.shape[0]
    reads_b = reads.reshape(count, STRETCH, -1).astype(jnp.float32)
    carried = jnp.einsum("btn,bhpn->bthp", reads_b, block_states, precision=highest)
    outputs = within + jnp.exp(cum_rate)[:, :, :, None] * carried
    return outputs.reshape(acts.shape)


def swapped(value, axis):
    count = lax.axis_size(axis)
    return lax.ppermute(value, axis, [(source, count - 1 - source) for source in range(count)])


def pick(values, index):
    chosen = values[0]
    for position in range(1, len(values)):
        chosen = jnp.where(index == position, values[position], chosen)
    return chosen


def block_at(blocks, chip, core):
    rows, width = blocks.shape[2], blocks.shape[3]
    return lax.dynamic_slice(blocks, (chip, core, 0, 0), (1, 1, rows, width))[0, 0]


def owned_rows(mixed, out_weight, residual):
    chips, cores = lax.axis_size("head_chip"), lax.axis_size("head_core")
    own_width = residual.shape[1]
    index = lax.axis_index("head_chip") * cores + lax.axis_index("head_core")
    own_block = jnp.arange(out_weight.shape[1]) // own_width == index
    repeats = out_weight.shape[1] // own_width

    def partial_of(rows, extra):
        value = jnp.dot(rows, out_weight, preferred_element_type=jnp.float32)
        spread = jnp.tile(extra.astype(jnp.float32), (1, repeats))
        return value + jnp.where(own_block[None, :], spread, 0.0)

    if chips != 2 or cores != 2:
        return lax.psum_scatter(
            partial_of(mixed, residual), ("head_chip", "head_core"), scatter_dimension=0, tiled=True
        )
    chip, core = lax.axis_index("head_chip"), lax.axis_index("head_core")
    rows = mixed.shape[0] // 4
    mixed4 = mixed.reshape(chips, cores, rows, -1)
    residual4 = residual.reshape(chips, cores, rows, -1)

    def part(at_chip, at_core):
        return partial_of(block_at(mixed4, at_chip, at_core), block_at(residual4, at_chip, at_core))

    far = part(1 - chip, core) + swapped(part(1 - chip, 1 - core), "head_core")
    arrived = swapped(far, "head_chip")
    near = part(chip, core) + swapped(part(chip, 1 - core), "head_core")
    return near + arrived


def project_all_rows(own, key_weight, value_weight):
    def project(rows):
        return (
            jnp.dot(rows, key_weight, preferred_element_type=jnp.float32).astype(jnp.bfloat16),
            jnp.dot(rows, value_weight, preferred_element_type=jnp.float32).astype(jnp.bfloat16),
        )

    chips, cores = lax.axis_size("head_chip"), lax.axis_size("head_core")
    if chips != 2 or cores != 2:
        return project(lax.all_gather(own, ("head_chip", "head_core"), axis=0, tiled=True))
    chip, core = lax.axis_index("head_chip"), lax.axis_index("head_core")
    other = swapped(own, "head_chip")
    partner = swapped(own, "head_core")
    partner_other = swapped(other, "head_core")
    results = [project(rows) for rows in (own, partner, other, partner_other)]
    assembled = []
    for which in range(2):
        own_p, partner_p, other_p, partner_other_p = (result[which] for result in results)
        near = pick([jnp.stack([own_p, partner_p]), jnp.stack([partner_p, own_p])], core)
        far = pick([jnp.stack([other_p, partner_other_p]), jnp.stack([partner_other_p, other_p])], core)
        whole = pick([jnp.stack([near, far]), jnp.stack([far, near])], chip)
        assembled.append(whole.reshape(-1, whole.shape[-1]))
    return tuple(assembled)


def per_device(
    inner_acts,
    gate_acts,
    write_map,
    read_map,
    step_raw,
    step_bias,
    decay_log,
    skip_gain,
    norm_gain,
    out_weight,
    residual,
    final_gain,
    key_weight,
    value_weight,
):
    tokens = inner_acts.shape[0]
    heads = step_bias.shape[0]
    width = inner_acts.shape[1] // heads
    acts = inner_acts.reshape(tokens, heads, width)
    decay_rate = -jnp.exp(decay_log)
    steps_fwd = jax.nn.softplus(step_raw[0] + step_bias[None, :])
    steps_bwd = jax.nn.softplus(step_raw[1] + step_bias[None, :])
    fwd_all = direction_out(
        acts, write_map[0], read_map[0], steps_fwd, steps_fwd * decay_rate[None, :], False, "seq"
    )
    bwd_all = direction_out(
        acts, write_map[1], read_map[1], steps_bwd, steps_bwd * decay_rate[None, :], True, "seq"
    )
    summed = fwd_all + bwd_all + skip_gain[None, :, None] * acts.astype(jnp.float32)
    summed = with_layout_constraint(summed.reshape(tokens, heads * width), Layout((0, 1)))
    gated = summed * jax.nn.silu(gate_acts.astype(jnp.float32))
    grouped = gated.reshape(tokens, NORM_GROUPS // (lax.axis_size("head_chip") * lax.axis_size("head_core")), -1)
    scaled = grouped * lax.rsqrt(jnp.mean(grouped * grouped, axis=2, keepdims=True) + epsilon)
    mixed = (scaled.reshape(tokens, -1) * norm_gain[None, :]).astype(jnp.bfloat16)
    encoded = owned_rows(mixed, out_weight, residual)
    normed = (
        encoded
        * lax.rsqrt(jnp.mean(encoded * encoded, axis=1, keepdims=True) + epsilon)
        * final_gain[None, :]
    ).astype(jnp.bfloat16)
    return project_all_rows(normed, key_weight, value_weight)


def split_head(mesh):
    shape = dict(mesh.shape)
    head = shape["head"]
    cores = 2 if head % 2 == 0 else 1
    devices = mesh.devices.reshape(shape["groups"], shape["seq"], head // cores, cores)
    return Mesh(devices, ("groups", "seq", "head_chip", "head_core"))


def solution(mesh):
    mesh = split_head(mesh)
    head = ("head_chip", "head_core")
    placed = (
        P(("groups", "seq"), head),
        P(("groups", "seq"), head),
        P(None, ("groups", "seq"), None),
        P(None, ("groups", "seq"), None),
        P(None, ("groups", "seq"), head),
        P(head),
        P(head),
        P(head),
        P(head),
        P(head, None),
        P(("groups", "seq"), head),
        P(),
        P(None, head),
        P(None, head),
    )
    return jax.shard_map(
        per_device,
        mesh=mesh,
        in_specs=placed,
        out_specs=(P(("groups", "seq"), head), P(("groups", "seq"), head)),
        check_vma=False,
    )
```

```python
import jax
import jax.numpy as jnp
from jax import lax
from jax.experimental.layout import Layout, with_layout_constraint
from jax.sharding import Mesh, PartitionSpec as P

STRETCH = 256
NORM_GROUPS = 4


epsilon = 1e-05
highest = lax.Precision.HIGHEST


def passed_along(value, axis, steps):
    count = lax.axis_size(axis)
    first, last = (max(0, -steps), min(count, count - steps))
    if first >= last:
        return jnp.zeros_like(value)
    return lax.ppermute(value, axis, [(source, source + steps) for source in range(first, last)])


def block_parts(acts, writes, reads, steps, rates, reverse):
    tokens, heads, width = acts.shape
    count = tokens // STRETCH
    acts_b = acts.reshape(count, STRETCH, heads, width)
    writes_b = writes.reshape(count, STRETCH, -1)
    reads_b = reads.reshape(count, STRETCH, -1)
    steps_b = steps.reshape(count, STRETCH, heads)
    rates_b = rates.reshape(count, STRETCH, heads)
    position = jnp.arange(STRETCH)
    if reverse:
        causal = position[:, None] <= position[None, :]
    else:
        causal = position[:, None] >= position[None, :]
    cum_rate = jnp.einsum(
        "ts,bsh->bth", causal.astype(jnp.float32), rates_b, precision=highest
    )
    block_total = cum_rate[:, 0] if reverse else cum_rate[:, -1]
    along = jnp.transpose(cum_rate, (0, 2, 1))
    spans = along[:, :, :, None] - along[:, :, None, :]
    decays = jnp.exp(jnp.where(causal[None, None], spans, -1e30))
    intersection = jnp.einsum("btn,bsn->bts", reads_b, writes_b, preferred_element_type=jnp.float32)
    weights = (
        intersection[:, None] * decays * jnp.transpose(steps_b, (0, 2, 1))[:, :, None, :]
    ).astype(jnp.bfloat16)
    within = jnp.einsum("bhts,bshp->bthp", weights, acts_b, preferred_element_type=jnp.float32)
    tail = jnp.exp(block_total[:, None, :] - cum_rate) * steps_b
    weighted = acts_b.astype(jnp.float32) * tail[:, :, :, None]
    ends = jnp.einsum(
        "bshp,bsn->bhpn", weighted, writes_b.astype(jnp.float32), precision=highest
    )
    return within, cum_rate, ends, jnp.exp(block_total)


def chain_blocks(ends, decays, reverse):
    count = ends.shape[0]
    order = range(count - 1, -1, -1) if reverse else range(count)
    state = jnp.zeros_like(ends[0])
    gain = jnp.ones_like(decays[0])
    starts = [None] * count
    gains = [None] * count
    for index in order:
        starts[index] = state
        gains[index] = gain
        state = decays[index][:, None, None] * state + ends[index]
        gain = gain * decays[index]
    return jnp.stack(starts), jnp.stack(gains), state, gain


def relay(state, gain, axis, steps):
    count = lax.axis_size(axis)
    if count <= 4:
        entering = jnp.zeros_like(state)
        for _ in range(count - 1):
            entering = passed_along(gain[:, None, None] * entering + state, axis, steps)
        return entering
    distance = 1
    while distance < count:
        got_state = passed_along(state, axis, distance * steps)
        got_gain = passed_along(gain, axis, distance * steps)
        state = gain[:, None, None] * got_state + state
        gain = gain * got_gain
        distance *= 2
    return passed_along(state, axis, steps)


def direction_out(acts, writes, reads, steps, rates, reverse, axis):
    within, cum_rate, ends, decays = block_parts(acts, writes, reads, steps, rates, reverse)
    starts, gains, own_end, own_gain = chain_blocks(ends, decays, reverse)
    entering = relay(own_end, own_gain, axis, -1 if reverse else 1)
    block_states = starts + gains[:, :, None, None] * entering[None]
    count = within.shape[0]
    reads_b = reads.reshape(count, STRETCH, -1).astype(jnp.float32)
    carried = jnp.einsum("btn,bhpn->bthp", reads_b, block_states, precision=highest)
    outputs = within + jnp.exp(cum_rate)[:, :, :, None] * carried
    return outputs.reshape(acts.shape)


def swapped(value, axis):
    count = lax.axis_size(axis)
    return lax.ppermute(value, axis, [(source, count - 1 - source) for source in range(count)])


def pick(values, index):
    chosen = values[0]
    for position in range(1, len(values)):
        chosen = jnp.where(index == position, values[position], chosen)
    return chosen


def block_at(blocks, chip, core):
    rows, width = blocks.shape[2], blocks.shape[3]
    return lax.dynamic_slice(blocks, (chip, core, 0, 0), (1, 1, rows, width))[0, 0]


def owned_rows(mixed, out_weight, residual):
    chips, cores = lax.axis_size("head_chip"), lax.axis_size("head_core")
    own_width = residual.shape[1]
    index = lax.axis_index("head_chip") * cores + lax.axis_index("head_core")
    own_block = jnp.arange(out_weight.shape[1]) // own_width == index
    repeats = out_weight.shape[1] // own_width

    def partial_of(rows, extra):
        value = jnp.dot(rows, out_weight, preferred_element_type=jnp.float32)
        spread = jnp.tile(extra.astype(jnp.float32), (1, repeats))
        return value + jnp.where(own_block[None, :], spread, 0.0)

    if chips != 2 or cores != 2:
        return lax.psum_scatter(
            partial_of(mixed, residual), ("head_chip", "head_core"), scatter_dimension=0, tiled=True
        )
    chip, core = lax.axis_index("head_chip"), lax.axis_index("head_core")
    rows = mixed.shape[0] // 4
    mixed4 = mixed.reshape(chips, cores, rows, -1)
    residual4 = residual.reshape(chips, cores, rows, -1)

    def part(at_chip, at_core):
        return partial_of(block_at(mixed4, at_chip, at_core), block_at(residual4, at_chip, at_core))

    far = part(1 - chip, core) + swapped(part(1 - chip, 1 - core), "head_core")
    arrived = swapped(far, "head_chip")
    near = part(chip, core) + swapped(part(chip, 1 - core), "head_core")
    return near + arrived


def project_all_rows(own, key_weight, value_weight):
    def project(rows):
        return (
            jnp.dot(rows, key_weight, preferred_element_type=jnp.float32).astype(jnp.bfloat16),
            jnp.dot(rows, value_weight, preferred_element_type=jnp.float32).astype(jnp.bfloat16),
        )

    chips, cores = lax.axis_size("head_chip"), lax.axis_size("head_core")
    if chips != 2 or cores != 2:
        return project(lax.all_gather(own, ("head_chip", "head_core"), axis=0, tiled=True))
    chip, core = lax.axis_index("head_chip"), lax.axis_index("head_core")
    other = swapped(own, "head_chip")
    partner = swapped(own, "head_core")
    partner_other = swapped(other, "head_core")
    results = [project(rows) for rows in (own, partner, other, partner_other)]
    assembled = []
    for which in range(2):
        own_p, partner_p, other_p, partner_other_p = (result[which] for result in results)
        stacked = jnp.stack([own_p, partner_p, other_p, partner_other_p])
        order = jnp.bitwise_xor(jnp.arange(4), chip * 2 + core)
        whole = jnp.take(stacked, order, axis=0)
        assembled.append(whole.reshape(-1, whole.shape[-1]))
    return tuple(assembled)


def per_device(
    inner_acts,
    gate_acts,
    write_map,
    read_map,
    step_raw,
    step_bias,
    decay_log,
    skip_gain,
    norm_gain,
    out_weight,
    residual,
    final_gain,
    key_weight,
    value_weight,
):
    tokens = inner_acts.shape[0]
    heads = step_bias.shape[0]
    width = inner_acts.shape[1] // heads
    acts = inner_acts.reshape(tokens, heads, width)
    decay_rate = -jnp.exp(decay_log)
    steps_fwd = jax.nn.softplus(step_raw[0] + step_bias[None, :])
    steps_bwd = jax.nn.softplus(step_raw[1] + step_bias[None, :])
    fwd_all = direction_out(
        acts, write_map[0], read_map[0], steps_fwd, steps_fwd * decay_rate[None, :], False, "seq"
    )
    bwd_all = direction_out(
        acts, write_map[1], read_map[1], steps_bwd, steps_bwd * decay_rate[None, :], True, "seq"
    )
    summed = fwd_all + bwd_all + skip_gain[None, :, None] * acts.astype(jnp.float32)
    summed = with_layout_constraint(summed.reshape(tokens, heads * width), Layout((0, 1)))
    gated = summed * jax.nn.silu(gate_acts.astype(jnp.float32))
    grouped = gated.reshape(tokens, NORM_GROUPS // (lax.axis_size("head_chip") * lax.axis_size("head_core")), -1)
    scaled = grouped * lax.rsqrt(jnp.mean(grouped * grouped, axis=2, keepdims=True) + epsilon)
    mixed = (scaled.reshape(tokens, -1) * norm_gain[None, :]).astype(jnp.bfloat16)
    encoded = owned_rows(mixed, out_weight, residual)
    normed = (
        encoded
        * lax.rsqrt(jnp.mean(encoded * encoded, axis=1, keepdims=True) + epsilon)
        * final_gain[None, :]
    ).astype(jnp.bfloat16)
    return project_all_rows(normed, key_weight, value_weight)


def split_head(mesh):
    shape = dict(mesh.shape)
    head = shape["head"]
    cores = 2 if head % 2 == 0 else 1
    devices = mesh.devices.reshape(shape["groups"], shape["seq"], head // cores, cores)
    return Mesh(devices, ("groups", "seq", "head_chip", "head_core"))


def solution(mesh):
    mesh = split_head(mesh)
    head = ("head_chip", "head_core")
    placed = (
        P(("groups", "seq"), head),
        P(("groups", "seq"), head),
        P(None, ("groups", "seq"), None),
        P(None, ("groups", "seq"), None),
        P(None, ("groups", "seq"), head),
        P(head),
        P(head),
        P(head),
        P(head),
        P(head, None),
        P(("groups", "seq"), head),
        P(),
        P(None, head),
        P(None, head),
    )
    return jax.shard_map(
        per_device,
        mesh=mesh,
        in_specs=placed,
        out_specs=(P(("groups", "seq"), head), P(("groups", "seq"), head)),
        check_vma=False,
    )
```

```python
import jax
import jax.numpy as jnp
from jax import lax
from jax.experimental.layout import Layout, with_layout_constraint
from jax.sharding import Mesh, PartitionSpec as P

STRETCH = 256
NORM_GROUPS = 4


epsilon = 1e-05
highest = lax.Precision.HIGHEST


def passed_along(value, axis, steps):
    count = lax.axis_size(axis)
    first, last = (max(0, -steps), min(count, count - steps))
    if first >= last:
        return jnp.zeros_like(value)
    return lax.ppermute(value, axis, [(source, source + steps) for source in range(first, last)])


def block_parts(acts, writes, reads, steps, rates, reverse):
    tokens, heads, width = acts.shape
    count = tokens // STRETCH
    acts_b = acts.reshape(count, STRETCH, heads, width)
    writes_b = writes.reshape(count, STRETCH, -1)
    reads_b = reads.reshape(count, STRETCH, -1)
    steps_b = steps.reshape(count, STRETCH, heads)
    rates_b = rates.reshape(count, STRETCH, heads)
    position = jnp.arange(STRETCH)
    if reverse:
        causal = position[:, None] <= position[None, :]
    else:
        causal = position[:, None] >= position[None, :]
    cum_rate = jnp.einsum(
        "ts,bsh->bth", causal.astype(jnp.float32), rates_b, precision=highest
    )
    block_total = cum_rate[:, 0] if reverse else cum_rate[:, -1]
    along = jnp.transpose(cum_rate, (0, 2, 1))
    spans = along[:, :, :, None] - along[:, :, None, :]
    decays = jnp.exp(jnp.where(causal[None, None], spans, -1e30))
    intersection = jnp.einsum("btn,bsn->bts", reads_b, writes_b, preferred_element_type=jnp.float32)
    weights = (
        intersection[:, None] * decays * jnp.transpose(steps_b, (0, 2, 1))[:, :, None, :]
    ).astype(jnp.bfloat16)
    within = jnp.einsum("bhts,bshp->bthp", weights, acts_b, preferred_element_type=jnp.float32)
    tail = jnp.exp(block_total[:, None, :] - cum_rate) * steps_b
    weighted = acts_b.astype(jnp.float32) * tail[:, :, :, None]
    ends = jnp.einsum(
        "bshp,bsn->bhpn", weighted, writes_b.astype(jnp.float32), precision=highest
    )
    return within, cum_rate, ends, jnp.exp(block_total)


def chain_blocks(ends, decays, reverse):
    count = ends.shape[0]
    order = range(count - 1, -1, -1) if reverse else range(count)
    state = jnp.zeros_like(ends[0])
    gain = jnp.ones_like(decays[0])
    starts = [None] * count
    gains = [None] * count
    for index in order:
        starts[index] = state
        gains[index] = gain
        state = decays[index][:, None, None] * state + ends[index]
        gain = gain * decays[index]
    return jnp.stack(starts), jnp.stack(gains), state, gain


def relay(state, gain, axis, steps):
    count = lax.axis_size(axis)
    if count <= 4:
        entering = jnp.zeros_like(state)
        for _ in range(count - 1):
            entering = passed_along(gain[:, None, None] * entering + state, axis, steps)
        return entering
    distance = 1
    while distance < count:
        got_state = passed_along(state, axis, distance * steps)
        got_gain = passed_along(gain, axis, distance * steps)
        state = gain[:, None, None] * got_state + state
        gain = gain * got_gain
        distance *= 2
    return passed_along(state, axis, steps)


def direction_out(acts, writes, reads, steps, rates, reverse, axis):
    within, cum_rate, ends, decays = block_parts(acts, writes, reads, steps, rates, reverse)
    starts, gains, own_end, own_gain = chain_blocks(ends, decays, reverse)
    entering = relay(own_end, own_gain, axis, -1 if reverse else 1)
    block_states = starts + gains[:, :, None, None] * entering[None]
    count = within.shape[0]
    reads_b = reads.reshape(count, STRETCH, -1).astype(jnp.float32)
    carried = jnp.einsum("btn,bhpn->bthp", reads_b, block_states, precision=highest)
    outputs = within + jnp.exp(cum_rate)[:, :, :, None] * carried
    return outputs.reshape(acts.shape)


def swapped(value, axis):
    count = lax.axis_size(axis)
    return lax.ppermute(value, axis, [(source, count - 1 - source) for source in range(count)])


def pick(values, index):
    chosen = values[0]
    for position in range(1, len(values)):
        chosen = jnp.where(index == position, values[position], chosen)
    return chosen


def block_at(blocks, chip, core):
    rows, width = blocks.shape[2], blocks.shape[3]
    return lax.dynamic_slice(blocks, (chip, core, 0, 0), (1, 1, rows, width))[0, 0]


def owned_rows(mixed, out_weight, residual):
    chips, cores = lax.axis_size("head_chip"), lax.axis_size("head_core")
    own_width = residual.shape[1]
    index = lax.axis_index("head_chip") * cores + lax.axis_index("head_core")
    own_block = jnp.arange(out_weight.shape[1]) // own_width == index
    repeats = out_weight.shape[1] // own_width

    def partial_of(rows, extra):
        value = jnp.dot(rows, out_weight, preferred_element_type=jnp.float32)
        window = lax.dynamic_slice_in_dim(value, index * own_width, own_width, 1)
        return lax.dynamic_update_slice_in_dim(
            value, window + extra.astype(jnp.float32), index * own_width, 1
        )

    if chips != 2 or cores != 2:
        return lax.psum_scatter(
            partial_of(mixed, residual), ("head_chip", "head_core"), scatter_dimension=0, tiled=True
        )
    chip, core = lax.axis_index("head_chip"), lax.axis_index("head_core")
    rows = mixed.shape[0] // 4
    mixed4 = mixed.reshape(chips, cores, rows, -1)
    residual4 = residual.reshape(chips, cores, rows, -1)

    def part(at_chip, at_core):
        return partial_of(block_at(mixed4, at_chip, at_core), block_at(residual4, at_chip, at_core))

    far = part(1 - chip, core) + swapped(part(1 - chip, 1 - core), "head_core")
    arrived = swapped(far, "head_chip")
    near = part(chip, core) + swapped(part(chip, 1 - core), "head_core")
    return near + arrived


def project_all_rows(own, key_weight, value_weight):
    def project(rows):
        return (
            jnp.dot(rows, key_weight, preferred_element_type=jnp.float32).astype(jnp.bfloat16),
            jnp.dot(rows, value_weight, preferred_element_type=jnp.float32).astype(jnp.bfloat16),
        )

    chips, cores = lax.axis_size("head_chip"), lax.axis_size("head_core")
    if chips != 2 or cores != 2:
        return project(lax.all_gather(own, ("head_chip", "head_core"), axis=0, tiled=True))
    chip, core = lax.axis_index("head_chip"), lax.axis_index("head_core")
    other = swapped(own, "head_chip")
    partner = swapped(own, "head_core")
    partner_other = swapped(other, "head_core")
    results = [project(rows) for rows in (own, partner, other, partner_other)]
    assembled = []
    for which in range(2):
        own_p, partner_p, other_p, partner_other_p = (result[which] for result in results)
        near = pick([jnp.stack([own_p, partner_p]), jnp.stack([partner_p, own_p])], core)
        far = pick([jnp.stack([other_p, partner_other_p]), jnp.stack([partner_other_p, other_p])], core)
        whole = pick([jnp.stack([near, far]), jnp.stack([far, near])], chip)
        assembled.append(whole.reshape(-1, whole.shape[-1]))
    return tuple(assembled)


def per_device(
    inner_acts,
    gate_acts,
    write_map,
    read_map,
    step_raw,
    step_bias,
    decay_log,
    skip_gain,
    norm_gain,
    out_weight,
    residual,
    final_gain,
    key_weight,
    value_weight,
):
    tokens = inner_acts.shape[0]
    heads = step_bias.shape[0]
    width = inner_acts.shape[1] // heads
    acts = inner_acts.reshape(tokens, heads, width)
    decay_rate = -jnp.exp(decay_log)
    steps_fwd = jax.nn.softplus(step_raw[0] + step_bias[None, :])
    steps_bwd = jax.nn.softplus(step_raw[1] + step_bias[None, :])
    fwd_all = direction_out(
        acts, write_map[0], read_map[0], steps_fwd, steps_fwd * decay_rate[None, :], False, "seq"
    )
    bwd_all = direction_out(
        acts, write_map[1], read_map[1], steps_bwd, steps_bwd * decay_rate[None, :], True, "seq"
    )
    summed = fwd_all + bwd_all + skip_gain[None, :, None] * acts.astype(jnp.float32)
    summed = with_layout_constraint(summed.reshape(tokens, heads * width), Layout((0, 1)))
    gated = summed * jax.nn.silu(gate_acts.astype(jnp.float32))
    grouped = gated.reshape(tokens, NORM_GROUPS // (lax.axis_size("head_chip") * lax.axis_size("head_core")), -1)
    scaled = grouped * lax.rsqrt(jnp.mean(grouped * grouped, axis=2, keepdims=True) + epsilon)
    mixed = (scaled.reshape(tokens, -1) * norm_gain[None, :]).astype(jnp.bfloat16)
    encoded = owned_rows(mixed, out_weight, residual)
    normed = (
        encoded
        * lax.rsqrt(jnp.mean(encoded * encoded, axis=1, keepdims=True) + epsilon)
        * final_gain[None, :]
    ).astype(jnp.bfloat16)
    return project_all_rows(normed, key_weight, value_weight)


def split_head(mesh):
    shape = dict(mesh.shape)
    head = shape["head"]
    cores = 2 if head % 2 == 0 else 1
    devices = mesh.devices.reshape(shape["groups"], shape["seq"], head // cores, cores)
    return Mesh(devices, ("groups", "seq", "head_chip", "head_core"))


def solution(mesh):
    mesh = split_head(mesh)
    head = ("head_chip", "head_core")
    placed = (
        P(("groups", "seq"), head),
        P(("groups", "seq"), head),
        P(None, ("groups", "seq"), None),
        P(None, ("groups", "seq"), None),
        P(None, ("groups", "seq"), head),
        P(head),
        P(head),
        P(head),
        P(head),
        P(head, None),
        P(("groups", "seq"), head),
        P(),
        P(None, head),
        P(None, head),
    )
    return jax.shard_map(
        per_device,
        mesh=mesh,
        in_specs=placed,
        out_specs=(P(("groups", "seq"), head), P(("groups", "seq"), head)),
        check_vma=False,
    )
```
